512 devices in a mesh: grp: 4 (over y), seq: 32 (over z, core), head: 4 (over x).
Axes of the slice: x: 4, y: 4, z: 16, core: 2. Of those that a mesh axis runs over, the one named last changes fastest.
Arguments:
- light_q: bfloat16 [16384, 4096], P(('grp', 'seq'), 'head'), may hold values from -6 to 6
- light_k: bfloat16 [16384, 4096], P(('grp', 'seq'), 'head'), may hold values from -6 to 6
- light_v: bfloat16 [16384, 4096], P(('grp', 'seq'), 'head'), may hold values from -6 to 6
- log_decay: float32 [32, 16384], P('head', ('grp', 'seq')), may hold values from -1 to 0
- light_gain: float32 [4096], P('head'), may hold values from 0.1 to 1.9
- soft_q: bfloat16 [16384, 8192], P(('grp', 'seq'), 'head'), may hold values from -5 to 5
- soft_k: bfloat16 [16384, 1024], P(('grp', 'seq'), 'head'), may hold values from -5 to 5
- soft_v: bfloat16 [16384, 1024], P(('grp', 'seq'), 'head'), may hold values from -6 to 6
- segment_ids: int32 [128], replicated, may hold values from 0 to 32, never falling along the last dimension, each value on 1 to 8 neighbouring positions
Outputs:
- light_out: bfloat16 [16384, 4096], P(('grp', 'seq'), 'head')
- soft_out: bfloat16 [16384, 8192], P(('grp', 'seq'), 'head')
The draws below stay inside these ranges and needn't reach their ends.
Inputs may be any that keep to these rules, and one draw needn't show every extreme that they name: `segment_ids`: segment numbers never fall along the sequence; each document covers 1 to 8 blocks, and one covers exactly 8.
All inputs are finite; a program needn't handle non-finite values.
Results may differ from the reference program's by a relative error of at most 0.0054.
Values may be sent and summed in bfloat16 or wider, within the bound.
No kernel may reach another device: no remote copies, remote signals or barrier semaphores. Data moves between devices by JAX's collectives and lax.ppermute only.
A program may use at most 192 MiB of HBM per device.

```python
import math
import jax
import jax.numpy as jnp
import numpy as np
from jax import lax

LIGHTNING_HEADS = 32
Q_HEADS = 64
KV_HEADS = 8
HEAD_DIM = 128
BLOCK = 128
TOK_DEV = 128
PACKED_TOKENS = 16384
SPAN = 8
NB = 128
MOST_BLOCKS = 8
DOCS = 33


def draw_log_decay(key, part):
    root_random_key = jax.random.fold_in(key, 11)
    variety_random_key, quick_random_key, gradual_random_key, machine_random_key, spike_random_key, layer_random_key = jax.random.split(root_random_key, 6)
    fast_head = jax.random.randint(variety_random_key, (LIGHTNING_HEADS, 1), 0, 2) == 0
    fast_rate = jnp.exp(jax.random.uniform(quick_random_key, (LIGHTNING_HEADS, 1), jnp.float32, math.log(1.0 / 50.0), math.log(1.0 / 30.0)))
    chain_len = MOST_BLOCKS * BLOCK
    slow_rate = jnp.exp(jax.random.uniform(gradual_random_key, (LIGHTNING_HEADS, 1), jnp.float32, math.log(0.05), math.log(0.4))) * (math.log(10.0) / chain_len)
    starting_decay_rate = jnp.where(fast_head, fast_rate, slow_rate)
    shard_count = PACKED_TOKENS // TOK_DEV
    multiplier = jnp.exp(jax.random.uniform(machine_random_key, (LIGHTNING_HEADS, shard_count), jnp.float32, -math.log(2.0), math.log(2.0)))
    multiplier = jnp.repeat(multiplier, TOK_DEV, axis=1)
    sudden_spike = jax.random.randint(spike_random_key, (LIGHTNING_HEADS, PACKED_TOKENS), 0, 1500) == 0
    layer_position = jax.random.uniform(layer_random_key, (LIGHTNING_HEADS, PACKED_TOKENS), jnp.float32, 0.22, 0.69)
    return (-(starting_decay_rate * multiplier) - jnp.where(sudden_spike, layer_position, 0.0)).astype(jnp.float32)


def soft_pair(key):
    root_random_key = jax.random.fold_in(key, 23)
    key_draw, query_draw = jax.random.split(root_random_key, 2)
    key_rows = jnp.clip(jax.random.normal(key_draw, (PACKED_TOKENS, KV_HEADS, HEAD_DIM), jnp.float32), -5.0, 5.0)
    query_rows = jnp.clip(jax.random.normal(query_draw, (PACKED_TOKENS, Q_HEADS, HEAD_DIM), jnp.float32), -5.0, 5.0)
    return (query_rows.reshape(PACKED_TOKENS, Q_HEADS * HEAD_DIM), key_rows.reshape(PACKED_TOKENS, KV_HEADS * HEAD_DIM))


def draw_soft_q(key, part):
    return soft_pair(key)[0].astype(jnp.bfloat16)


def draw_soft_k(key, part):
    return soft_pair(key)[1].astype(jnp.bfloat16)


def block_levels(rng, dims, pieces, smallest, high):
    loudness, own = 1.0, jax.random.fold_in(rng, 6)
    for axis_at, parts in pieces:
        heights = jnp.exp(jax.random.uniform(jax.random.fold_in(own, axis_at), (parts,), jnp.float32, smallest / len(pieces), high / len(pieces)))
        loudness = loudness * jnp.repeat(heights, dims[axis_at] // parts).reshape([-1 if axis == axis_at else 1 for axis in range(len(dims))])
    return loudness


def profile(count, total, reach, lean):
    loads = [(1 << 20) // math.isqrt(standing ** lean) + 1 for standing in range(2, count + 1)]
    spare, counts = total - reach - (count - 1), [1] * (count - 1)
    while spare > 0:
        free = [i for i in range(count - 1) if counts[i] < reach]
        pool, left = sum([loads[i] for i in free]), spare
        for i in free:
            more = min(reach - counts[i], max(1, left * loads[i] // pool), spare)
            counts[i] = counts[i] + more
            spare = spare - more
    return np.array([reach] + counts)


def ragged(key, number_of, total, bound, skew):
    if number_of == 2:
        one = jax.random.randint(key, (), max(1, total - bound), min(bound, total - 1) + 1)
        return jnp.stack([one, total - one])
    lengths = jnp.asarray(profile(number_of, total, bound, skew), jnp.int32)
    pairs = (number_of - 1) // 2
    giver, sink = lengths[1:1 + 2 * pairs:2], lengths[2:2 + 2 * pairs:2]
    margin = jnp.minimum(giver - 1, bound - sink)
    shifted = jax.random.randint(jax.random.fold_in(key, 1), (pairs,), 0, 1 << 20) % (margin + 1)
    lengths = lengths.at[1:1 + 2 * pairs:2].set(giver - shifted).at[2:2 + 2 * pairs:2].set(sink + shifted)
    return lengths[jax.random.permutation(jax.random.fold_in(key, 2), number_of)]


def noise(own_key, extent, width, bound, shards=(), kind=jnp.bfloat16):
    loudness = block_levels(own_key, extent, shards, -0.22, 0.18) if shards else 1.0
    entries = jax.random.normal(own_key, extent, jnp.float32) * width * loudness
    return jnp.minimum(jnp.maximum(entries, -bound), bound).astype(kind)


def setup_inputs(seed: int = 0) -> dict:
    key_of = jax.random.split(jax.random.key(seed), 10)
    light_q = noise(key_of[0], (PACKED_TOKENS, LIGHTNING_HEADS * HEAD_DIM), 1.0, 6.0, ((0, 128), (1, 4)))
    light_k = noise(key_of[1], (PACKED_TOKENS, LIGHTNING_HEADS * HEAD_DIM), 1.0, 6.0, ((0, 128), (1, 4)))
    light_v = noise(key_of[2], (PACKED_TOKENS, LIGHTNING_HEADS * HEAD_DIM), 1.0, 6.0, ((0, 128), (1, 4)))
    log_decay = draw_log_decay(jax.random.fold_in(key_of[9], 71), 0)
    light_gain = jnp.clip(1.0 + 0.18 * jax.random.normal(key_of[4], (LIGHTNING_HEADS * HEAD_DIM,), jnp.float32), 0.1, 1.9)
    soft_q = draw_soft_q(jax.random.fold_in(key_of[9], 71), 0)
    soft_k = draw_soft_k(jax.random.fold_in(key_of[9], 71), 0)
    soft_v = noise(key_of[7], (PACKED_TOKENS, KV_HEADS * HEAD_DIM), 1.0, 6.0, ((0, 128), (1, 4)))
    segment_ids = jnp.searchsorted(jnp.cumsum(ragged(key_of[8], DOCS, NB, MOST_BLOCKS, 0)), jnp.arange(NB), side="right").astype(jnp.int32)
    return dict(light_q=light_q, light_k=light_k, light_v=light_v, log_decay=log_decay, light_gain=light_gain, soft_q=soft_q, soft_k=soft_k, soft_v=soft_v, segment_ids=segment_ids)


NEG_FLOOR = -10000.0
MASK_FILL = -1e+30
TOP_PRECISION = lax.Precision.HIGHEST

def rounded_copy(array):
    return lax.optimization_barrier(array.astype(jnp.bfloat16)).astype(jnp.float32)

def light_block(q_block, k_block, v_block, decay_block, seg_block, prev_last):
    tok_rows = q_block.shape[0]
    q_float = q_block.astype(jnp.float32)
    k_float = k_block.astype(jnp.float32)
    v_float = v_block.astype(jnp.float32)
    levels = jnp.cumsum(decay_block, axis=1)
    offsets = jnp.arange(tok_rows, dtype=jnp.int32)
    allowed = (offsets[:, None] >= offsets[None, :]) & (seg_block[:, None] == seg_block[None, :])
    decays = jnp.exp(jnp.where(allowed[None], levels[:, :, None] - levels[:, None, :], NEG_FLOOR))
    scores = jnp.einsum('thd,shd->hts', q_float, k_float, precision=TOP_PRECISION)
    weights = rounded_copy(scores * decays)
    intra_part = jnp.einsum('hts,shd->thd', weights, v_float, precision=TOP_PRECISION)
    last_seg = seg_block[tok_rows - 1]
    tail_gain = jnp.exp(jnp.where((seg_block == last_seg)[None, :], levels[:, tok_rows - 1:tok_rows] - levels, NEG_FLOOR))
    keyed = rounded_copy(k_float * tail_gain.T[:, :, None])
    local_state = jnp.einsum('shd,she->hde', keyed, v_float, precision=TOP_PRECISION)
    first_seg = seg_block[0]
    joined = (first_seg == prev_last) & jnp.all(seg_block == first_seg)
    carry_gain = jnp.where(joined, jnp.exp(levels[:, tok_rows - 1]), 0.0)
    reach_gain = jnp.where(((seg_block == first_seg) & (first_seg == prev_last))[None, :], jnp.exp(levels), 0.0)
    return (intra_part, carry_gain, local_state, reach_gain, q_float)

def lightning(light_q, light_k, light_v, log_decay, light_gain, seg_all):
    num_blocks = PACKED_TOKENS // TOK_DEV
    q_blocks = light_q.reshape(num_blocks, TOK_DEV, LIGHTNING_HEADS, HEAD_DIM)
    k_blocks = light_k.reshape(num_blocks, TOK_DEV, LIGHTNING_HEADS, HEAD_DIM)
    v_blocks = light_v.reshape(num_blocks, TOK_DEV, LIGHTNING_HEADS, HEAD_DIM)
    decay_blocks = log_decay.reshape(LIGHTNING_HEADS, num_blocks, TOK_DEV).transpose(1, 0, 2)
    seg_blocks = seg_all.reshape(num_blocks, TOK_DEV)
    prev_segs = jnp.concatenate([jnp.array([-1], jnp.int32), seg_blocks[:-1, -1]])

    def advance(state, inputs):
        q_block, k_block, v_block, decay_block, seg_block, prev_last = inputs
        intra_part, carry_gain, local_state, reach_gain, q_float = light_block(q_block, k_block, v_block, decay_block, seg_block, prev_last)
        state_rounded = rounded_copy(state)
        inter_part = jnp.einsum('thd,hde->the', q_float, state_rounded, precision=TOP_PRECISION) * reach_gain.T[:, :, None]
        new_state = carry_gain[:, None, None] * state + local_state
        return (new_state, intra_part + inter_part)
    start_state = jnp.zeros((LIGHTNING_HEADS, HEAD_DIM, HEAD_DIM), jnp.float32)
    _, mixed = lax.scan(advance, start_state, (q_blocks, k_blocks, v_blocks, decay_blocks, seg_blocks, prev_segs))
    mixed = mixed.reshape(PACKED_TOKENS, LIGHTNING_HEADS * HEAD_DIM)
    mean_square = lax.optimization_barrier(jnp.mean(mixed * mixed, axis=1, keepdims=True))
    return (mixed * lax.rsqrt(mean_square + 1e-06) * light_gain).astype(jnp.bfloat16)

def softmax_layer(soft_q, soft_k, soft_v, seg_all):
    num_blocks = PACKED_TOKENS // TOK_DEV
    group_size = Q_HEADS // KV_HEADS
    front = (SPAN - 1) * TOK_DEV
    key_pad = jnp.concatenate([jnp.zeros((front, KV_HEADS * HEAD_DIM), soft_k.dtype), soft_k])
    value_pad = jnp.concatenate([jnp.zeros((front, KV_HEADS * HEAD_DIM), soft_v.dtype), soft_v])
    seg_pad = jnp.concatenate([jnp.full((front,), -1, jnp.int32), seg_all])

    def one_block(device):
        row_start = (device * TOK_DEV).astype(jnp.int32)
        q_float = lax.dynamic_slice_in_dim(soft_q, row_start, TOK_DEV).astype(jnp.float32).reshape(TOK_DEV, KV_HEADS, group_size, HEAD_DIM)
        k_float = lax.dynamic_slice_in_dim(key_pad, row_start, SPAN * TOK_DEV).astype(jnp.float32).reshape(SPAN * TOK_DEV, KV_HEADS, HEAD_DIM)
        v_float = lax.dynamic_slice_in_dim(value_pad, row_start, SPAN * TOK_DEV).astype(jnp.float32).reshape(SPAN * TOK_DEV, KV_HEADS, HEAD_DIM)
        query_seg = lax.dynamic_slice_in_dim(seg_all, row_start, TOK_DEV)
        key_seg = lax.dynamic_slice_in_dim(seg_pad, row_start, SPAN * TOK_DEV)
        query_pos = row_start + jnp.arange(TOK_DEV, dtype=jnp.int32)
        key_pos = row_start - front + jnp.arange(SPAN * TOK_DEV, dtype=jnp.int32)
        allowed = (key_pos[None, :] <= query_pos[:, None]) & (key_seg[None, :] == query_seg[:, None])
        scores = jnp.einsum('tkgd,skd->tkgs', q_float, k_float, precision=TOP_PRECISION) * HEAD_DIM ** (-0.5)
        scores = jnp.where(allowed[:, None, None, :], scores, MASK_FILL)
        row_max = lax.optimization_barrier(jnp.max(scores, axis=-1, keepdims=True))
        exponent = jnp.exp(scores - row_max)
        weights = rounded_copy(exponent)
        output = jnp.einsum('tkgs,skd->tkgd', weights, v_float, precision=TOP_PRECISION) / lax.optimization_barrier(jnp.sum(exponent, axis=-1))[..., None]
        return output.reshape(TOK_DEV, Q_HEADS * HEAD_DIM).astype(jnp.bfloat16)
    blocks_out = lax.map(one_block, jnp.arange(num_blocks, dtype=jnp.int32))
    return blocks_out.reshape(PACKED_TOKENS, Q_HEADS * HEAD_DIM)

def reference(light_q, light_k, light_v, log_decay, light_gain, soft_q, soft_k, soft_v, segment_ids):
    seg_all = jnp.repeat(segment_ids, BLOCK)
    light_out = lightning(light_q, light_k, light_v, log_decay, light_gain, seg_all)
    soft_out = softmax_layer(soft_q, soft_k, soft_v, seg_all)
    return (light_out, soft_out)
```

```python
from functools import partial

import jax
import jax.numpy as jnp
from jax import lax
from jax.sharding import PartitionSpec as P

LIGHTNING_HEADS = 32
HEAD_DIM = 128
BLOCK = 128
WINDOW_DEV = 8


NEG_FLOOR = -10000.0
MASK_FILL = -1e30


def prefix(x, axis, combine, identity):
    count, here = (lax.axis_size(axis), lax.axis_index(axis))
    everything = jax.tree.map(lambda part: lax.all_gather(part, axis), x)
    start = jax.tree.map(
        lambda part, zero: jnp.broadcast_to(jnp.asarray(zero, part.dtype), part.shape), x, identity
    )

    def lap(k, before):
        reached = k < here
        new = combine(before, jax.tree.map(lambda part: part[k], everything))
        return jax.tree.map(lambda a, b: jnp.where(reached, a, b), new, before)

    return lax.fori_loop(0, count, lap, start)


def from_behind(x, axis, by):
    count = lax.axis_size(axis)
    pairs = [(i, i + by) for i in range(count) if 0 <= i + by < count]
    return lax.ppermute(x, axis, pairs)


def window_scan(x, axis, width):
    reach = 1
    while reach < min(width, lax.axis_size(axis)):
        x = join_states(jax.tree.map(lambda part: from_behind(part, axis, reach), x), x)
        reach *= 2
    return x


def join_states(earlier, later):
    return (earlier[0] * later[0], earlier[1] * later[0][:, None, None] + later[1])


def token_segments(segment_ids, row_start, tok_rows):
    blocks = lax.dynamic_slice_in_dim(segment_ids, row_start // BLOCK, tok_rows // BLOCK)
    return jnp.repeat(blocks, BLOCK)


def lightning_local(light_q, light_k, light_v, log_decay, seg_tok, prev_last):
    tok_rows, feat_width = light_q.shape
    head_count = feat_width // HEAD_DIM
    queries = light_q.reshape(tok_rows, head_count, HEAD_DIM)
    key_rows = light_k.reshape(tok_rows, head_count, HEAD_DIM)
    value_rows = light_v.reshape(tok_rows, head_count, HEAD_DIM)
    levels = jnp.cumsum(log_decay, axis=1)
    offsets = jnp.arange(tok_rows, dtype=jnp.int32)
    allowed = (offsets[:, None] >= offsets[None, :]) & (seg_tok[:, None] == seg_tok[None, :])
    decays = jnp.exp(jnp.where(allowed[None], levels[:, :, None] - levels[:, None, :], NEG_FLOOR))
    scores = jnp.einsum("thd,shd->hts", queries, key_rows, preferred_element_type=jnp.float32)
    weights = (scores * decays).astype(jnp.bfloat16)
    intra_part = jnp.einsum("hts,shd->thd", weights, value_rows, preferred_element_type=jnp.float32)
    last_seg = seg_tok[tok_rows - 1]
    tail_gain = jnp.exp(
        jnp.where(
            (seg_tok == last_seg)[None, :], levels[:, tok_rows - 1 : tok_rows] - levels, NEG_FLOOR
        )
    )
    keyed = (key_rows * tail_gain.T[:, :, None]).astype(jnp.bfloat16)
    local_state = jnp.einsum("shd,she->hde", keyed, value_rows, preferred_element_type=jnp.float32)
    first_seg = seg_tok[0]
    joined = (first_seg == prev_last) & jnp.all(seg_tok == first_seg)
    carry_gain = jnp.where(joined, jnp.exp(levels[:, tok_rows - 1]), 0.0)
    reach_gain = jnp.where(
        ((seg_tok == first_seg) & (first_seg == prev_last))[None, :], jnp.exp(levels), 0.0
    )
    return (intra_part, (carry_gain, local_state), reach_gain, queries)


def absorb(running, queries, key_rows, value_rows, allowed):
    row_max, row_mass, weighted = running
    scores = jnp.einsum(
        "tkgd,skd->tkgs", queries, key_rows, preferred_element_type=jnp.float32
    ) * HEAD_DIM ** (-0.5)
    scores = jnp.where(allowed[:, None, None, :], scores, MASK_FILL)
    new_max = jnp.maximum(row_max, jnp.max(scores, axis=-1))
    exponent = jnp.exp(scores - new_max[..., None])
    shrink = jnp.exp(row_max - new_max)
    row_mass = row_mass * shrink + jnp.sum(exponent, axis=-1)
    update = jnp.einsum(
        "tkgs,skd->tkgd",
        exponent.astype(jnp.bfloat16),
        value_rows,
        preferred_element_type=jnp.float32,
    )
    weighted = weighted * shrink[..., None] + update
    return (new_max, row_mass, weighted)


def body(light_q, light_k, light_v, log_decay, light_gain, soft_q, soft_k, soft_v, segment_ids):
    tok_rows = light_q.shape[0]
    position = lax.axis_index(("grp", "seq"))
    row_start = position * tok_rows
    seg_tok = token_segments(segment_ids, row_start, tok_rows)
    prev_index = jnp.maximum(position * (tok_rows // BLOCK) - 1, 0)
    prev_last = jnp.where(
        position > 0, lax.dynamic_index_in_dim(segment_ids, prev_index, keepdims=False), -1
    )
    intra_part, element, reach_gain, queries = lightning_local(
        light_q, light_k, light_v, log_decay, seg_tok, prev_last
    )
    reach = window_scan(element, ("grp", "seq"), WINDOW_DEV)
    entering = from_behind(reach[1], ("grp", "seq"), 1)
    state_rounded = entering.astype(jnp.bfloat16)
    inter_part = (
        jnp.einsum("thd,hde->the", queries, state_rounded, preferred_element_type=jnp.float32)
        * reach_gain.T[:, :, None]
    )
    mixed = (intra_part + inter_part).reshape(tok_rows, -1)
    square_sum = lax.psum(jnp.sum(mixed * mixed, axis=1), "head")
    inv_norm = lax.rsqrt(square_sum / (LIGHTNING_HEADS * HEAD_DIM) + 1e-06)
    light_out = (mixed * inv_norm[:, None] * light_gain).astype(jnp.bfloat16)
    kv_pair = jnp.stack([soft_k, soft_v])
    window_len = min(WINDOW_DEV, lax.axis_size(("grp", "seq")))

    window = kv_pair[None]
    while window.shape[0] < window_len:
        window = jnp.concatenate(
            [window, from_behind(window, ("grp", "seq"), window.shape[0])]
        )[:window_len]
    kv_heads = soft_k.shape[1] // HEAD_DIM
    group_size = soft_q.shape[1] // soft_k.shape[1]
    soft_queries = soft_q.reshape(tok_rows, kv_heads, group_size, HEAD_DIM)
    query_pos = row_start + jnp.arange(tok_rows, dtype=jnp.int32)
    slots_per = max(1, 512 // tok_rows)
    running = (
        jnp.full((tok_rows, kv_heads, group_size), MASK_FILL, jnp.float32),
        jnp.zeros((tok_rows, kv_heads, group_size), jnp.float32),
        jnp.zeros((tok_rows, kv_heads, group_size, HEAD_DIM), jnp.float32),
    )
    for first_slot in range(0, window_len, slots_per):
        slot_list = list(range(first_slot, min(first_slot + slots_per, window_len)))
        chosen = window[first_slot : first_slot + len(slot_list)]
        key_rows = chosen[:, 0].reshape(-1, kv_heads, HEAD_DIM)
        value_rows = chosen[:, 1].reshape(-1, kv_heads, HEAD_DIM)
        key_pos = jnp.concatenate(
            [
                (position - source) * tok_rows + jnp.arange(tok_rows, dtype=jnp.int32)
                for source in slot_list
            ]
        )
        key_seg = jnp.concatenate(
            [
                token_segments(segment_ids, jnp.maximum(position - source, 0) * tok_rows, tok_rows)
                for source in slot_list
            ]
        )
        allowed = (
            (key_pos[None, :] <= query_pos[:, None])
            & (key_pos >= 0)[None, :]
            & (key_seg[None, :] == seg_tok[:, None])
        )
        step_fn = partial(
            absorb, queries=soft_queries, key_rows=key_rows, value_rows=value_rows, allowed=allowed
        )
        running = step_fn(running)
    row_max, row_mass, weighted = running
    soft_out = (weighted / row_mass[..., None]).reshape(tok_rows, -1).astype(jnp.bfloat16)
    return (light_out, soft_out)


def solution(mesh):
    placed = (
        P(("grp", "seq"), "head"),
        P(("grp", "seq"), "head"),
        P(("grp", "seq"), "head"),
        P("head", ("grp", "seq")),
        P("head"),
        P(("grp", "seq"), "head"),
        P(("grp", "seq"), "head"),
        P(("grp", "seq"), "head"),
        P(),
    )
    return jax.shard_map(
        body,
        mesh=mesh,
        in_specs=placed,
        out_specs=(P(("grp", "seq"), "head"), P(("grp", "seq"), "head")),
        check_vma=False,
    )
```

```python
from functools import partial

import jax
import jax.numpy as jnp
from jax import lax
from jax.sharding import PartitionSpec as P

LIGHTNING_HEADS = 32
HEAD_DIM = 128
BLOCK = 128
WINDOW_DEV = 8


NEG_FLOOR = -10000.0
MASK_FILL = -1e30


def from_behind(x, axis, by):
    count = lax.axis_size(axis)
    pairs = [(i, i + by) for i in range(count) if 0 <= i + by < count]
    return lax.ppermute(x, axis, pairs)


def shift_pairs(count, by, parity=None):
    return [
        (i, i + by)
        for i in range(count)
        if 0 <= i + by < count and (parity is None or i % 2 == parity)
    ]


def move(x, axis, pairs):
    return jax.tree.map(lambda part: lax.ppermute(part, axis, pairs), x)


def state_entering(element, axis, core):
    count = lax.axis_size(axis)
    pair = join_states(move(element, axis, shift_pairs(count, 1, 0)), element)
    wide = pair
    for chips in (1, 2):
        wide = join_states(move(wide, axis, shift_pairs(count, 2 * chips, 1)), wide)
    before = move(wide[1], axis, shift_pairs(count, 1, 1))
    after = (before * element[0][:, None, None] + element[1]).astype(jnp.bfloat16)
    after = lax.ppermute(after, axis, shift_pairs(count, 1, 0))
    return jnp.where(core == 0, before.astype(jnp.bfloat16), after)


def kv_window(kv_pair, axis, core, width):
    count = lax.axis_size(axis)
    ring = [kv_pair]
    for step in range(1, width // 2 + 1):
        parity = 1 if step == width // 2 else None
        ring.append(lax.ppermute(ring[-1], axis, shift_pairs(count, 2, parity)))
    half = width // 2
    mine = jnp.stack(ring[:half])
    sent = jnp.where(core == 1, jnp.stack(ring[1 : half + 1]), mine)
    swap = [(i, i ^ 1) for i in range(count)]
    theirs = lax.ppermute(sent, axis, swap)
    return jnp.stack([mine, theirs], axis=1).reshape((width,) + kv_pair.shape)


def join_states(earlier, later):
    return (earlier[0] * later[0], earlier[1] * later[0][:, None, None] + later[1])


def token_segments(segment_ids, row_start, tok_rows):
    blocks = lax.dynamic_slice_in_dim(segment_ids, row_start // BLOCK, tok_rows // BLOCK)
    return jnp.repeat(blocks, BLOCK)


def lightning_local(light_q, light_k, light_v, log_decay, seg_tok, prev_last):
    tok_rows, feat_width = light_q.shape
    head_count = feat_width // HEAD_DIM
    queries = light_q.reshape(tok_rows, head_count, HEAD_DIM)
    key_rows = light_k.reshape(tok_rows, head_count, HEAD_DIM)
    value_rows = light_v.reshape(tok_rows, head_count, HEAD_DIM)
    levels = jnp.cumsum(log_decay, axis=1)
    offsets = jnp.arange(tok_rows, dtype=jnp.int32)
    allowed = (offsets[:, None] >= offsets[None, :]) & (seg_tok[:, None] == seg_tok[None, :])
    decays = jnp.exp(jnp.where(allowed[None], levels[:, :, None] - levels[:, None, :], NEG_FLOOR))
    scores = jnp.einsum("thd,shd->hts", queries, key_rows, preferred_element_type=jnp.float32)
    weights = (scores * decays).astype(jnp.bfloat16)
    intra_part = jnp.einsum("hts,shd->thd", weights, value_rows, preferred_element_type=jnp.float32)
    last_seg = seg_tok[tok_rows - 1]
    tail_gain = jnp.exp(
        jnp.where(
            (seg_tok == last_seg)[None, :], levels[:, tok_rows - 1 : tok_rows] - levels, NEG_FLOOR
        )
    )
    keyed = (key_rows * tail_gain.T[:, :, None]).astype(jnp.bfloat16)
    local_state = jnp.einsum("shd,she->hde", keyed, value_rows, preferred_element_type=jnp.float32)
    first_seg = seg_tok[0]
    joined = (first_seg == prev_last) & jnp.all(seg_tok == first_seg)
    carry_gain = jnp.where(joined, jnp.exp(levels[:, tok_rows - 1]), 0.0)
    reach_gain = jnp.where(
        ((seg_tok == first_seg) & (first_seg == prev_last))[None, :], jnp.exp(levels), 0.0
    )
    return (intra_part, (carry_gain, local_state), reach_gain, queries)


def absorb(running, queries, key_rows, value_rows, allowed):
    row_max, row_mass, weighted = running
    scores = jnp.einsum(
        "tkgd,skd->tkgs", queries, key_rows, preferred_element_type=jnp.float32
    ) * HEAD_DIM ** (-0.5)
    scores = jnp.where(allowed[:, None, None, :], scores, MASK_FILL)
    new_max = jnp.maximum(row_max, jnp.max(scores, axis=-1))
    exponent = jnp.exp(scores - new_max[..., None])
    shrink = jnp.exp(row_max - new_max)
    row_mass = row_mass * shrink + jnp.sum(exponent, axis=-1)
    update = jnp.einsum(
        "tkgs,skd->tkgd",
        exponent.astype(jnp.bfloat16),
        value_rows,
        preferred_element_type=jnp.float32,
    )
    weighted = weighted * shrink[..., None] + update
    return (new_max, row_mass, weighted)


def body(light_q, light_k, light_v, log_decay, light_gain, soft_q, soft_k, soft_v, segment_ids):
    tok_rows = light_q.shape[0]
    position = lax.axis_index(("grp", "seq"))
    row_start = position * tok_rows
    seg_tok = token_segments(segment_ids, row_start, tok_rows)
    prev_index = jnp.maximum(position * (tok_rows // BLOCK) - 1, 0)
    prev_last = jnp.where(
        position > 0, lax.dynamic_index_in_dim(segment_ids, prev_index, keepdims=False), -1
    )
    intra_part, element, reach_gain, queries = lightning_local(
        light_q, light_k, light_v, log_decay, seg_tok, prev_last
    )
    core = position % 2
    state_rounded = state_entering(element, ("grp", "seq"), core)
    inter_part = (
        jnp.einsum("thd,hde->the", queries, state_rounded, preferred_element_type=jnp.float32)
        * reach_gain.T[:, :, None]
    )
    mixed = (intra_part + inter_part).reshape(tok_rows, -1)
    square_sum = lax.psum(jnp.sum(mixed * mixed, axis=1), "head")
    inv_norm = lax.rsqrt(square_sum / (LIGHTNING_HEADS * HEAD_DIM) + 1e-06)
    light_out = (mixed * inv_norm[:, None] * light_gain).astype(jnp.bfloat16)
    kv_pair = jnp.stack([soft_k, soft_v])
    window_len = min(WINDOW_DEV, lax.axis_size(("grp", "seq")))

    window = kv_window(kv_pair, ("grp", "seq"), core, window_len)
    kv_heads = soft_k.shape[1] // HEAD_DIM
    group_size = soft_q.shape[1] // soft_k.shape[1]
    soft_queries = soft_q.reshape(tok_rows, kv_heads, group_size, HEAD_DIM)
    query_pos = row_start + jnp.arange(tok_rows, dtype=jnp.int32)
    slots_per = max(1, 512 // tok_rows)
    running = (
        jnp.full((tok_rows, kv_heads, group_size), MASK_FILL, jnp.float32),
        jnp.zeros((tok_rows, kv_heads, group_size), jnp.float32),
        jnp.zeros((tok_rows, kv_heads, group_size, HEAD_DIM), jnp.float32),
    )
    for first_slot in range(0, window_len, slots_per):
        slot_list = list(range(first_slot, min(first_slot + slots_per, window_len)))
        chosen = window[first_slot : first_slot + len(slot_list)]
        key_rows = chosen[:, 0].reshape(-1, kv_heads, HEAD_DIM)
        value_rows = chosen[:, 1].reshape(-1, kv_heads, HEAD_DIM)
        key_pos = jnp.concatenate(
            [
                (position - source) * tok_rows + jnp.arange(tok_rows, dtype=jnp.int32)
                for source in slot_list
            ]
        )
        key_seg = jnp.concatenate(
            [
                token_segments(segment_ids, jnp.maximum(position - source, 0) * tok_rows, tok_rows)
                for source in slot_list
            ]
        )
        allowed = (
            (key_pos[None, :] <= query_pos[:, None])
            & (key_pos >= 0)[None, :]
            & (key_seg[None, :] == seg_tok[:, None])
        )
        step_fn = partial(
            absorb, queries=soft_queries, key_rows=key_rows, value_rows=value_rows, allowed=allowed
        )
        running = step_fn(running)
    row_max, row_mass, weighted = running
    soft_out = (weighted / row_mass[..., None]).reshape(tok_rows, -1).astype(jnp.bfloat16)
    return (light_out, soft_out)


def solution(mesh):
    placed = (
        P(("grp", "seq"), "head"),
        P(("grp", "seq"), "head"),
        P(("grp", "seq"), "head"),
        P("head", ("grp", "seq")),
        P("head"),
        P(("grp", "seq"), "head"),
        P(("grp", "seq"), "head"),
        P(("grp", "seq"), "head"),
        P(),
    )
    return jax.shard_map(
        body,
        mesh=mesh,
        in_specs=placed,
        out_specs=(P(("grp", "seq"), "head"), P(("grp", "seq"), "head")),
        check_vma=False,
    )
```

```python
from functools import partial

import jax
import jax.numpy as jnp
from jax import lax
from jax.sharding import PartitionSpec as P

LIGHTNING_HEADS = 32
HEAD_DIM = 128
BLOCK = 128
WINDOW_DEV = 8


NEG_FLOOR = -10000.0
MASK_FILL = -1e30


def shift_pairs(count, by, parity=None):
    return [
        (i, i + by)
        for i in range(count)
        if 0 <= i + by < count and (parity is None or i % 2 == parity)
    ]


def move(x, axis, pairs):
    return jax.tree.map(lambda part: lax.ppermute(part, axis, pairs), x)


def exchange(element, kv_pair, axis, core, width):
    count = lax.axis_size(axis)
    half = width // 2
    ring = [kv_pair]

    def ring_step(parity=None):
        return lax.ppermute(ring[-1], axis, shift_pairs(count, 2, parity))

    got = move(element, axis, shift_pairs(count, 1, 0))
    got, kv_next = lax.optimization_barrier((got, ring_step()))
    ring.append(kv_next)
    wide = join_states(got, element)
    got = move(wide, axis, shift_pairs(count, 2, 1))
    got, kv_next = lax.optimization_barrier((got, ring_step()))
    ring.append(kv_next)
    wide = join_states(got, wide)
    got = lax.ppermute(wide[1], axis, shift_pairs(count, 4, 1))
    got, kv_next = lax.optimization_barrier((got, ring_step()))
    ring.append(kv_next)
    wide_state = got * wide[0][:, None, None] + wide[1]
    before = lax.ppermute(wide_state, axis, shift_pairs(count, 1, 1))
    before, kv_next = lax.optimization_barrier((before, ring_step(1)))
    ring.append(kv_next)
    after = (before * element[0][:, None, None] + element[1]).astype(jnp.bfloat16)
    after = lax.ppermute(after, axis, shift_pairs(count, 1, 0))
    mine = jnp.stack(ring[:half])
    sent = jnp.where(core == 1, jnp.stack(ring[1 : half + 1]), mine)
    theirs = lax.ppermute(sent, axis, [(i, i ^ 1) for i in range(count)])
    state = jnp.where(core == 0, before.astype(jnp.bfloat16), after)
    return state, mine, theirs


def join_states(earlier, later):
    return (earlier[0] * later[0], earlier[1] * later[0][:, None, None] + later[1])


def token_segments(segment_ids, row_start, tok_rows):
    blocks = lax.dynamic_slice_in_dim(segment_ids, row_start // BLOCK, tok_rows // BLOCK)
    return jnp.repeat(blocks, BLOCK)


def lightning_local(light_q, light_k, light_v, log_decay, seg_tok, prev_last):
    tok_rows, feat_width = light_q.shape
    head_count = feat_width // HEAD_DIM
    queries = light_q.reshape(tok_rows, head_count, HEAD_DIM)
    key_rows = light_k.reshape(tok_rows, head_count, HEAD_DIM)
    value_rows = light_v.reshape(tok_rows, head_count, HEAD_DIM)
    levels = jnp.cumsum(log_decay, axis=1)
    offsets = jnp.arange(tok_rows, dtype=jnp.int32)
    allowed = (offsets[:, None] >= offsets[None, :]) & (seg_tok[:, None] == seg_tok[None, :])
    decays = jnp.exp(jnp.where(allowed[None], levels[:, :, None] - levels[:, None, :], NEG_FLOOR))
    scores = jnp.einsum("thd,shd->hts", queries, key_rows, preferred_element_type=jnp.float32)
    weights = (scores * decays).astype(jnp.bfloat16)
    intra_part = jnp.einsum("hts,shd->thd", weights, value_rows, preferred_element_type=jnp.float32)
    last_seg = seg_tok[tok_rows - 1]
    tail_gain = jnp.exp(
        jnp.where(
            (seg_tok == last_seg)[None, :], levels[:, tok_rows - 1 : tok_rows] - levels, NEG_FLOOR
        )
    )
    keyed = (key_rows * tail_gain.T[:, :, None]).astype(jnp.bfloat16)
    local_state = jnp.einsum("shd,she->hde", keyed, value_rows, preferred_element_type=jnp.float32)
    first_seg = seg_tok[0]
    joined = (first_seg == prev_last) & jnp.all(seg_tok == first_seg)
    carry_gain = jnp.where(joined, jnp.exp(levels[:, tok_rows - 1]), 0.0)
    reach_gain = jnp.where(
        ((seg_tok == first_seg) & (first_seg == prev_last))[None, :], jnp.exp(levels), 0.0
    )
    return (intra_part, (carry_gain, local_state), reach_gain, queries)


def absorb(running, queries, key_rows, value_rows, allowed):
    row_max, row_mass, weighted = running
    scores = jnp.einsum(
        "tkgd,skd->tkgs", queries, key_rows, preferred_element_type=jnp.float32
    ) * HEAD_DIM ** (-0.5)
    scores = jnp.where(allowed[:, None, None, :], scores, MASK_FILL)
    new_max = jnp.maximum(row_max, jnp.max(scores, axis=-1))
    exponent = jnp.exp(scores - new_max[..., None])
    shrink = jnp.exp(row_max - new_max)
    row_mass = row_mass * shrink + jnp.sum(exponent, axis=-1)
    update = jnp.einsum(
        "tkgs,skd->tkgd",
        exponent.astype(jnp.bfloat16),
        value_rows,
        preferred_element_type=jnp.float32,
    )
    weighted = weighted * shrink[..., None] + update
    return (new_max, row_mass, weighted)


def body(light_q, light_k, light_v, log_decay, light_gain, soft_q, soft_k, soft_v, segment_ids):
    tok_rows = light_q.shape[0]
    position = lax.axis_index(("grp", "seq"))
    row_start = position * tok_rows
    seg_tok = token_segments(segment_ids, row_start, tok_rows)
    prev_index = jnp.maximum(position * (tok_rows // BLOCK) - 1, 0)
    prev_last = jnp.where(
        position > 0, lax.dynamic_index_in_dim(segment_ids, prev_index, keepdims=False), -1
    )
    intra_part, element, reach_gain, queries = lightning_local(
        light_q, light_k, light_v, log_decay, seg_tok, prev_last
    )
    core = position % 2
    window_len = WINDOW_DEV
    state_rounded, mine, theirs = exchange(
        element, jnp.stack([soft_k, soft_v]), ("grp", "seq"), core, window_len
    )
    inter_part = (
        jnp.einsum("thd,hde->the", queries, state_rounded, preferred_element_type=jnp.float32)
        * reach_gain.T[:, :, None]
    )
    mixed = (intra_part + inter_part).reshape(tok_rows, -1)
    square_sum = lax.psum(jnp.sum(mixed * mixed, axis=1), "head")
    inv_norm = lax.rsqrt(square_sum / (LIGHTNING_HEADS * HEAD_DIM) + 1e-06)
    light_out = (mixed * inv_norm[:, None] * light_gain).astype(jnp.bfloat16)
    kv_heads = soft_k.shape[1] // HEAD_DIM
    group_size = soft_q.shape[1] // soft_k.shape[1]
    soft_queries = soft_q.reshape(tok_rows, kv_heads, group_size, HEAD_DIM)
    query_pos = row_start + jnp.arange(tok_rows, dtype=jnp.int32)
    running = (
        jnp.full((tok_rows, kv_heads, group_size), MASK_FILL, jnp.float32),
        jnp.zeros((tok_rows, kv_heads, group_size), jnp.float32),
        jnp.zeros((tok_rows, kv_heads, group_size, HEAD_DIM), jnp.float32),
    )
    for slot_list, chosen in ((range(0, window_len, 2), mine), (range(1, window_len, 2), theirs)):
        key_rows = chosen[:, 0].reshape(-1, kv_heads, HEAD_DIM)
        value_rows = chosen[:, 1].reshape(-1, kv_heads, HEAD_DIM)
        key_pos = jnp.concatenate(
            [
                (position - source) * tok_rows + jnp.arange(tok_rows, dtype=jnp.int32)
                for source in slot_list
            ]
        )
        key_seg = jnp.concatenate(
            [
                token_segments(segment_ids, jnp.maximum(position - source, 0) * tok_rows, tok_rows)
                for source in slot_list
            ]
        )
        allowed = (
            (key_pos[None, :] <= query_pos[:, None])
            & (key_pos >= 0)[None, :]
            & (key_seg[None, :] == seg_tok[:, None])
        )
        step_fn = partial(
            absorb, queries=soft_queries, key_rows=key_rows, value_rows=value_rows, allowed=allowed
        )
        running = step_fn(running)
    row_max, row_mass, weighted = running
    soft_out = (weighted / row_mass[..., None]).reshape(tok_rows, -1).astype(jnp.bfloat16)
    return (light_out, soft_out)


def solution(mesh):
    placed = (
        P(("grp", "seq"), "head"),
        P(("grp", "seq"), "head"),
        P(("grp", "seq"), "head"),
        P("head", ("grp", "seq")),
        P("head"),
        P(("grp", "seq"), "head"),
        P(("grp", "seq"), "head"),
        P(("grp", "seq"), "head"),
        P(),
    )
    return jax.shard_map(
        body,
        mesh=mesh,
        in_specs=placed,
        out_specs=(P(("grp", "seq"), "head"), P(("grp", "seq"), "head")),
        check_vma=False,
    )
```

```python
import jax
import jax.numpy as jnp
from jax import lax
from jax.sharding import PartitionSpec as P

LIGHTNING_HEADS = 32
HEAD_DIM = 128
BLOCK = 128
WINDOW_DEV = 8


NEG_FLOOR = -10000.0
MASK_FILL = -1e30


def shift_pairs(count, by, parity=None):
    return [
        (i, i + by)
        for i in range(count)
        if 0 <= i + by < count and (parity is None or i % 2 == parity)
    ]


def move(x, axis, pairs):
    return jax.tree.map(lambda part: lax.ppermute(part, axis, pairs), x)


def exchange(element, kv_pair, axis, core, width, take, running):
    count = lax.axis_size(axis)
    half = width // 2
    swap = [(i, i ^ 1) for i in range(count)]
    ring = [kv_pair]

    def ring_step(parity=None):
        return lax.ppermute(ring[-1], axis, shift_pairs(count, 2, parity))

    got = move(element, axis, shift_pairs(count, 1, 0))
    got, kv_next = lax.optimization_barrier((got, ring_step()))
    ring.append(kv_next)
    wide = join_states(got, element)
    got = move(wide, axis, shift_pairs(count, 2, 1))
    got, kv_next = lax.optimization_barrier((got, ring_step()))
    ring.append(kv_next)
    wide = join_states(got, wide)
    got = lax.ppermute(wide[1], axis, shift_pairs(count, 4, 1))
    got, kv_next = lax.optimization_barrier((got, ring_step()))
    ring.append(kv_next)
    wide_state = got * wide[0][:, None, None] + wide[1]
    mine = jnp.stack(ring[:half])
    sent = jnp.where(core == 1, jnp.stack(ring[1:half]), jnp.stack(ring[: half - 1]))
    running = take(running, range(0, width, 2), mine)
    before = lax.ppermute(wide_state, axis, shift_pairs(count, 1, 1))
    before, kv_next, theirs, running = lax.optimization_barrier(
        (before, ring_step(1), lax.ppermute(sent, axis, swap), running)
    )
    ring.append(kv_next)
    last = jnp.where(core == 1, ring[half], ring[half - 1])
    running = take(running, range(1, width - 2, 2), theirs)
    after = (before * element[0][:, None, None] + element[1]).astype(jnp.bfloat16)
    after, last, running = lax.optimization_barrier(
        (
            lax.ppermute(after, axis, shift_pairs(count, 1, 0)),
            lax.ppermute(last, axis, swap),
            running,
        )
    )
    running = take(running, [width - 1], last[None])
    state = jnp.where(core == 0, before.astype(jnp.bfloat16), after)
    return state, running


def sum_over(x, axis):
    count, here = (lax.axis_size(axis), lax.axis_index(axis))
    parts = [x] + [
        lax.ppermute(x, axis, [(i, (i + by) % count) for i in range(count)])
        for by in range(1, count)
    ]
    ordered = jnp.take(jnp.stack(parts), (here - jnp.arange(count)) % count, axis=0)
    total = ordered[0]
    for k in range(1, count):
        total = total + ordered[k]
    return total


def join_states(earlier, later):
    return (earlier[0] * later[0], earlier[1] * later[0][:, None, None] + later[1])


def token_segments(segment_ids, row_start, tok_rows):
    blocks = lax.dynamic_slice_in_dim(segment_ids, row_start // BLOCK, tok_rows // BLOCK)
    return jnp.repeat(blocks, BLOCK)


def lightning_local(light_q, light_k, light_v, log_decay, seg_tok, prev_last):
    tok_rows, feat_width = light_q.shape
    head_count = feat_width // HEAD_DIM
    queries = light_q.reshape(tok_rows, head_count, HEAD_DIM)
    key_rows = light_k.reshape(tok_rows, head_count, HEAD_DIM)
    value_rows = light_v.reshape(tok_rows, head_count, HEAD_DIM)
    levels = jnp.cumsum(log_decay, axis=1)
    offsets = jnp.arange(tok_rows, dtype=jnp.int32)
    allowed = (offsets[:, None] >= offsets[None, :]) & (seg_tok[:, None] == seg_tok[None, :])
    decays = jnp.exp(jnp.where(allowed[None], levels[:, :, None] - levels[:, None, :], NEG_FLOOR))
    scores = jnp.einsum("thd,shd->hts", queries, key_rows, preferred_element_type=jnp.float32)
    weights = (scores * decays).astype(jnp.bfloat16)
    intra_part = jnp.einsum("hts,shd->thd", weights, value_rows, preferred_element_type=jnp.float32)
    last_seg = seg_tok[tok_rows - 1]
    tail_gain = jnp.exp(
        jnp.where(
            (seg_tok == last_seg)[None, :], levels[:, tok_rows - 1 : tok_rows] - levels, NEG_FLOOR
        )
    )
    keyed = (key_rows * tail_gain.T[:, :, None]).astype(jnp.bfloat16)
    local_state = jnp.einsum("shd,she->hde", keyed, value_rows, preferred_element_type=jnp.float32)
    first_seg = seg_tok[0]
    joined = (first_seg == prev_last) & jnp.all(seg_tok == first_seg)
    carry_gain = jnp.where(joined, jnp.exp(levels[:, tok_rows - 1]), 0.0)
    reach_gain = jnp.where(
        ((seg_tok == first_seg) & (first_seg == prev_last))[None, :], jnp.exp(levels), 0.0
    )
    return (intra_part, (carry_gain, local_state), reach_gain, queries)


def absorb(running, queries, key_rows, value_rows, allowed):
    row_max, row_mass, weighted = running
    scores = jnp.einsum(
        "tkgd,skd->tkgs", queries, key_rows, preferred_element_type=jnp.float32
    ) * HEAD_DIM ** (-0.5)
    scores = jnp.where(allowed[:, None, None, :], scores, MASK_FILL)
    new_max = jnp.maximum(row_max, jnp.max(scores, axis=-1))
    exponent = jnp.exp(scores - new_max[..., None])
    shrink = jnp.exp(row_max - new_max)
    row_mass = row_mass * shrink + jnp.sum(exponent, axis=-1)
    update = jnp.einsum(
        "tkgs,skd->tkgd",
        exponent.astype(jnp.bfloat16),
        value_rows,
        preferred_element_type=jnp.float32,
    )
    weighted = weighted * shrink[..., None] + update
    return (new_max, row_mass, weighted)


def body(light_q, light_k, light_v, log_decay, light_gain, soft_q, soft_k, soft_v, segment_ids):
    tok_rows = light_q.shape[0]
    position = lax.axis_index(("grp", "seq"))
    row_start = position * tok_rows
    seg_tok = token_segments(segment_ids, row_start, tok_rows)
    prev_index = jnp.maximum(position * (tok_rows // BLOCK) - 1, 0)
    prev_last = jnp.where(
        position > 0, lax.dynamic_index_in_dim(segment_ids, prev_index, keepdims=False), -1
    )
    intra_part, element, reach_gain, queries = lightning_local(
        light_q, light_k, light_v, log_decay, seg_tok, prev_last
    )
    core = position % 2
    window_len = WINDOW_DEV
    kv_heads = soft_k.shape[1] // HEAD_DIM
    group_size = soft_q.shape[1] // soft_k.shape[1]
    soft_queries = soft_q.reshape(tok_rows, kv_heads, group_size, HEAD_DIM)
    query_pos = row_start + jnp.arange(tok_rows, dtype=jnp.int32)

    def take(running, slot_list, chosen):
        key_rows = chosen[:, 0].reshape(-1, kv_heads, HEAD_DIM)
        value_rows = chosen[:, 1].reshape(-1, kv_heads, HEAD_DIM)
        key_pos = jnp.concatenate(
            [
                (position - source) * tok_rows + jnp.arange(tok_rows, dtype=jnp.int32)
                for source in slot_list
            ]
        )
        key_seg = jnp.concatenate(
            [
                token_segments(segment_ids, jnp.maximum(position - source, 0) * tok_rows, tok_rows)
                for source in slot_list
            ]
        )
        allowed = (
            (key_pos[None, :] <= query_pos[:, None])
            & (key_pos >= 0)[None, :]
            & (key_seg[None, :] == seg_tok[:, None])
        )
        return absorb(running, soft_queries, key_rows, value_rows, allowed)

    running = (
        jnp.full((tok_rows, kv_heads, group_size), MASK_FILL, jnp.float32),
        jnp.zeros((tok_rows, kv_heads, group_size), jnp.float32),
        jnp.zeros((tok_rows, kv_heads, group_size, HEAD_DIM), jnp.float32),
    )
    state_rounded, running = exchange(
        element, jnp.stack([soft_k, soft_v]), ("grp", "seq"), core, window_len, take, running
    )
    inter_part = (
        jnp.einsum("thd,hde->the", queries, state_rounded, preferred_element_type=jnp.float32)
        * reach_gain.T[:, :, None]
    )
    mixed = (intra_part + inter_part).reshape(tok_rows, -1)
    square_sum = sum_over(jnp.sum(mixed * mixed, axis=1), "head")
    inv_norm = lax.rsqrt(square_sum / (LIGHTNING_HEADS * HEAD_DIM) + 1e-06)
    light_out = (mixed * inv_norm[:, None] * light_gain).astype(jnp.bfloat16)
    row_max, row_mass, weighted = running
    soft_out = (weighted / row_mass[..., None]).reshape(tok_rows, -1).astype(jnp.bfloat16)
    return (light_out, soft_out)


def solution(mesh):
    placed = (
        P(("grp", "seq"), "head"),
        P(("grp", "seq"), "head"),
        P(("grp", "seq"), "head"),
        P("head", ("grp", "seq")),
        P("head"),
        P(("grp", "seq"), "head"),
        P(("grp", "seq"), "head"),
        P(("grp", "seq"), "head"),
        P(),
    )
    return jax.shard_map(
        body,
        mesh=mesh,
        in_specs=placed,
        out_specs=(P(("grp", "seq"), "head"), P(("grp", "seq"), "head")),
        check_vma=False,
    )
```

```python
import jax
import jax.numpy as jnp
from jax import lax
from jax.sharding import PartitionSpec as P

LIGHTNING_HEADS = 32
HEAD_DIM = 128
BLOCK = 128
WINDOW_DEV = 8


NEG_FLOOR = -10000.0
MASK_FILL = -1e30


def shift_pairs(count, by, parity=None):
    return [
        (i, i + by)
        for i in range(count)
        if 0 <= i + by < count and (parity is None or i % 2 == parity)
    ]


def exchange(element, kv_pair, axis, core, width, take, running):
    count = lax.axis_size(axis)
    half = width // 2
    swap = [(i, i ^ 1) for i in range(count)]
    ring = [kv_pair]

    def ring_step(parity=None):
        return lax.ppermute(ring[-1], axis, shift_pairs(count, 2, parity))

    gain, state = element
    rows = state.shape[1]
    packed = jnp.concatenate([state, jnp.broadcast_to(gain[:, None, None], state[:, :1].shape)], 1)
    got = lax.ppermute(packed, axis, shift_pairs(count, 1, 0))
    got, kv_next = lax.optimization_barrier((got, ring_step()))
    ring.append(kv_next)
    wide_state = got[:, :rows] * gain[:, None, None] + state
    wide_gain = got[:, rows, 0] * gain
    high = wide_gain.astype(jnp.bfloat16)
    low = (wide_gain - high.astype(jnp.float32)).astype(jnp.bfloat16)
    packed = jnp.concatenate(
        [
            wide_state.astype(jnp.bfloat16),
            jnp.broadcast_to(high[:, None, None], state[:, :1].shape),
            jnp.broadcast_to(low[:, None, None], state[:, :1].shape),
        ],
        1,
    )
    got = lax.ppermute(packed, axis, shift_pairs(count, 2, 1))
    got, kv_next = lax.optimization_barrier((got, ring_step()))
    ring.append(kv_next)
    got_gain = got[:, rows, 0].astype(jnp.float32) + got[:, rows + 1, 0].astype(jnp.float32)
    wide_state = got[:, :rows].astype(jnp.float32) * wide_gain[:, None, None] + wide_state
    wide_gain = got_gain * wide_gain
    got = lax.ppermute(wide_state.astype(jnp.bfloat16), axis, shift_pairs(count, 4, 1))
    got, kv_next = lax.optimization_barrier((got, ring_step()))
    ring.append(kv_next)
    wide_state = got.astype(jnp.float32) * wide_gain[:, None, None] + wide_state
    mine = jnp.stack(ring[:half])
    sent = jnp.where(core == 1, jnp.stack(ring[1:half]), jnp.stack(ring[: half - 1]))
    running = take(running, range(0, width, 2), mine)
    before = lax.ppermute(wide_state.astype(jnp.bfloat16), axis, shift_pairs(count, 1, 1))
    before, kv_next, theirs, running = lax.optimization_barrier(
        (before, ring_step(1), lax.ppermute(sent, axis, swap), running)
    )
    ring.append(kv_next)
    last = jnp.where(core == 1, ring[half], ring[half - 1])
    running = take(running, range(1, width - 2, 2), theirs)
    after = (before.astype(jnp.float32) * gain[:, None, None] + state).astype(jnp.bfloat16)
    after, last, running = lax.optimization_barrier(
        (
            lax.ppermute(after, axis, shift_pairs(count, 1, 0)),
            lax.ppermute(last, axis, swap),
            running,
        )
    )
    running = take(running, [width - 1], last[None])
    return jnp.where(core == 0, before, after), running


def token_segments(segment_ids, row_start, tok_rows):
    blocks = lax.dynamic_slice_in_dim(segment_ids, row_start // BLOCK, tok_rows // BLOCK)
    return jnp.repeat(blocks, BLOCK)


def lightning_local(light_q, light_k, light_v, log_decay, seg_tok, prev_last):
    tok_rows, feat_width = light_q.shape
    head_count = feat_width // HEAD_DIM
    queries = light_q.reshape(tok_rows, head_count, HEAD_DIM)
    key_rows = light_k.reshape(tok_rows, head_count, HEAD_DIM)
    value_rows = light_v.reshape(tok_rows, head_count, HEAD_DIM)
    levels = jnp.cumsum(log_decay, axis=1)
    offsets = jnp.arange(tok_rows, dtype=jnp.int32)
    allowed = (offsets[:, None] >= offsets[None, :]) & (seg_tok[:, None] == seg_tok[None, :])
    decays = jnp.exp(jnp.where(allowed[None], levels[:, :, None] - levels[:, None, :], NEG_FLOOR))
    scores = jnp.einsum("thd,shd->hts", queries, key_rows, preferred_element_type=jnp.float32)
    weights = (scores * decays).astype(jnp.bfloat16)
    intra_part = jnp.einsum("hts,shd->thd", weights, value_rows, preferred_element_type=jnp.float32)
    last_seg = seg_tok[tok_rows - 1]
    tail_gain = jnp.exp(
        jnp.where(
            (seg_tok == last_seg)[None, :], levels[:, tok_rows - 1 : tok_rows] - levels, NEG_FLOOR
        )
    )
    keyed = (key_rows * tail_gain.T[:, :, None]).astype(jnp.bfloat16)
    local_state = jnp.einsum("shd,she->hde", keyed, value_rows, preferred_element_type=jnp.float32)
    first_seg = seg_tok[0]
    joined = (first_seg == prev_last) & jnp.all(seg_tok == first_seg)
    carry_gain = jnp.where(joined, jnp.exp(levels[:, tok_rows - 1]), 0.0)
    reach_gain = jnp.where(
        ((seg_tok == first_seg) & (first_seg == prev_last))[None, :], jnp.exp(levels), 0.0
    )
    return (intra_part, (carry_gain, local_state), reach_gain, queries)


def absorb(running, queries, key_rows, value_rows, allowed):
    row_max, row_mass, weighted = running
    scores = jnp.einsum(
        "tkgd,skd->tkgs", queries, key_rows, preferred_element_type=jnp.float32
    ) * HEAD_DIM ** (-0.5)
    scores = jnp.where(allowed[:, None, None, :], scores, MASK_FILL)
    new_max = jnp.maximum(row_max, jnp.max(scores, axis=-1))
    exponent = jnp.exp(scores - new_max[..., None])
    shrink = jnp.exp(row_max - new_max)
    row_mass = row_mass * shrink + jnp.sum(exponent, axis=-1)
    update = jnp.einsum(
        "tkgs,skd->tkgd",
        exponent.astype(jnp.bfloat16),
        value_rows,
        preferred_element_type=jnp.float32,
    )
    weighted = weighted * shrink[..., None] + update
    return (new_max, row_mass, weighted)


def body(light_q, light_k, light_v, log_decay, light_gain, soft_q, soft_k, soft_v, segment_ids):
    tok_rows = light_q.shape[0]
    position = lax.axis_index(("grp", "seq"))
    row_start = position * tok_rows
    seg_tok = token_segments(segment_ids, row_start, tok_rows)
    prev_index = jnp.maximum(position * (tok_rows // BLOCK) - 1, 0)
    prev_last = jnp.where(
        position > 0, lax.dynamic_index_in_dim(segment_ids, prev_index, keepdims=False), -1
    )
    intra_part, element, reach_gain, queries = lightning_local(
        light_q, light_k, light_v, log_decay, seg_tok, prev_last
    )
    core = position % 2
    window_len = WINDOW_DEV
    kv_heads = soft_k.shape[1] // HEAD_DIM
    group_size = soft_q.shape[1] // soft_k.shape[1]
    soft_queries = soft_q.reshape(tok_rows, kv_heads, group_size, HEAD_DIM)
    query_pos = row_start + jnp.arange(tok_rows, dtype=jnp.int32)

    def take(running, slot_list, chosen):
        key_rows = chosen[:, 0].reshape(-1, kv_heads, HEAD_DIM)
        value_rows = chosen[:, 1].reshape(-1, kv_heads, HEAD_DIM)
        key_pos = jnp.concatenate(
            [
                (position - source) * tok_rows + jnp.arange(tok_rows, dtype=jnp.int32)
                for source in slot_list
            ]
        )
        key_seg = jnp.concatenate(
            [
                token_segments(segment_ids, jnp.maximum(position - source, 0) * tok_rows, tok_rows)
                for source in slot_list
            ]
        )
        allowed = (
            (key_pos[None, :] <= query_pos[:, None])
            & (key_pos >= 0)[None, :]
            & (key_seg[None, :] == seg_tok[:, None])
        )
        return absorb(running, soft_queries, key_rows, value_rows, allowed)

    running = (
        jnp.full((tok_rows, kv_heads, group_size), MASK_FILL, jnp.float32),
        jnp.zeros((tok_rows, kv_heads, group_size), jnp.float32),
        jnp.zeros((tok_rows, kv_heads, group_size, HEAD_DIM), jnp.float32),
    )
    state_rounded, running = exchange(
        element, jnp.stack([soft_k, soft_v]), ("grp", "seq"), core, window_len, take, running
    )
    inter_part = (
        jnp.einsum("thd,hde->the", queries, state_rounded, preferred_element_type=jnp.float32)
        * reach_gain.T[:, :, None]
    )
    mixed = (intra_part + inter_part).reshape(tok_rows, -1)
    square_sum = lax.psum(jnp.sum(mixed * mixed, axis=1), "head")
    inv_norm = lax.rsqrt(square_sum / (LIGHTNING_HEADS * HEAD_DIM) + 1e-06)
    light_out = (mixed * inv_norm[:, None] * light_gain).astype(jnp.bfloat16)
    row_max, row_mass, weighted = running
    soft_out = (weighted / row_mass[..., None]).reshape(tok_rows, -1).astype(jnp.bfloat16)
    return (light_out, soft_out)


def solution(mesh):
    placed = (
        P(("grp", "seq"), "head"),
        P(("grp", "seq"), "head"),
        P(("grp", "seq"), "head"),
        P("head", ("grp", "seq")),
        P("head"),
        P(("grp", "seq"), "head"),
        P(("grp", "seq"), "head"),
        P(("grp", "seq"), "head"),
        P(),
    )
    return jax.shard_map(
        body,
        mesh=mesh,
        in_specs=placed,
        out_specs=(P(("grp", "seq"), "head"), P(("grp", "seq"), "head")),
        check_vma=False,
    )
```

```python
import jax
import jax.numpy as jnp
from jax import lax
from jax.sharding import PartitionSpec as P

LIGHTNING_HEADS = 32
HEAD_DIM = 128
BLOCK = 128
WINDOW_DEV = 8


NEG_FLOOR = -10000.0
MASK_FILL = -1e30


def shift_pairs(count, by, parity=None):
    return [
        (i, i + by)
        for i in range(count)
        if 0 <= i + by < count and (parity is None or i % 2 == parity)
    ]


def exchange(element, kv_pair, axis, core, width, take, running):
    count = lax.axis_size(axis)
    swap = [(i, i ^ 1) for i in range(count)]
    ring = [kv_pair]

    def ring_step():
        return lax.ppermute(ring[-1], axis, shift_pairs(count, 2))

    gain, state = element
    rows = state.shape[1]
    row_of = lambda v: jnp.broadcast_to(v[:, None, None], state[:, :1].shape)
    packed = jnp.concatenate([state, row_of(gain)], 1)
    partner, kv_next = lax.optimization_barrier(
        (lax.ppermute(packed, axis, shift_pairs(count, 1, 0)), ring_step())
    )
    ring.append(kv_next)
    partner_state, partner_gain = partner[:, :rows], partner[:, rows, 0]
    wide_state = partner_state * gain[:, None, None] + state
    wide_gain = partner_gain * gain
    high = wide_gain.astype(jnp.bfloat16)
    low = (wide_gain - high.astype(jnp.float32)).astype(jnp.bfloat16)
    packed = jnp.concatenate([wide_state.astype(jnp.bfloat16), row_of(high), row_of(low)], 1)
    got, kv_next = lax.optimization_barrier(
        (lax.ppermute(packed, axis, shift_pairs(count, 2, 1)), ring_step())
    )
    ring.append(kv_next)
    got_gain = got[:, rows, 0].astype(jnp.float32) + got[:, rows + 1, 0].astype(jnp.float32)
    wide_state = got[:, :rows].astype(jnp.float32) * wide_gain[:, None, None] + wide_state
    wide_gain = got_gain * wide_gain
    sent = jnp.where(core == 1, jnp.stack(ring[1:3]), jnp.stack(ring[0:2]))
    running = take(running, [0, 2, 4], jnp.stack(ring[0:3]))
    got, kv_next, theirs, running = lax.optimization_barrier(
        (
            lax.ppermute(wide_state.astype(jnp.bfloat16), axis, shift_pairs(count, 4, 1)),
            ring_step(),
            lax.ppermute(sent, axis, swap),
            running,
        )
    )
    ring.append(kv_next)
    outgoing = (got.astype(jnp.float32) * wide_gain[:, None, None] + wide_state).astype(jnp.bfloat16)
    cross = jnp.concatenate([outgoing.reshape(-1, HEAD_DIM), ring[3].reshape(-1, HEAD_DIM)])
    sent = jnp.where(core == 1, jnp.stack([ring[3], ring[3]]), jnp.stack(ring[2:4]))
    running = take(running, [6, 1, 3], jnp.concatenate([ring[3][None], theirs]))
    cross, ahead, theirs, running = lax.optimization_barrier(
        (
            lax.ppermute(cross, axis, shift_pairs(count, 1, 1)),
            lax.ppermute(outgoing, axis, shift_pairs(count, 2, 1)),
            lax.ppermute(sent, axis, swap),
            running,
        )
    )
    split = outgoing.size // HEAD_DIM
    behind = cross[:split].reshape(outgoing.shape)
    after = ahead.astype(jnp.float32) * partner_gain[:, None, None] + partner_state
    last = jnp.where(
        core == 0, jnp.stack([theirs[0], cross[split:].reshape(kv_pair.shape)]), theirs
    )
    running = take(running, [5, 7], last)
    return jnp.where(core == 0, behind, after.astype(jnp.bfloat16)), running


def token_segments(segment_ids, row_start, tok_rows):
    blocks = lax.dynamic_slice_in_dim(segment_ids, row_start // BLOCK, tok_rows // BLOCK)
    return jnp.repeat(blocks, BLOCK)


def lightning_local(light_q, light_k, light_v, log_decay, seg_tok, prev_last):
    tok_rows, feat_width = light_q.shape
    head_count = feat_width // HEAD_DIM
    queries = light_q.reshape(tok_rows, head_count, HEAD_DIM)
    key_rows = light_k.reshape(tok_rows, head_count, HEAD_DIM)
    value_rows = light_v.reshape(tok_rows, head_count, HEAD_DIM)
    levels = jnp.cumsum(log_decay, axis=1)
    offsets = jnp.arange(tok_rows, dtype=jnp.int32)
    allowed = (offsets[:, None] >= offsets[None, :]) & (seg_tok[:, None] == seg_tok[None, :])
    decays = jnp.exp(jnp.where(allowed[None], levels[:, :, None] - levels[:, None, :], NEG_FLOOR))
    scores = jnp.einsum("thd,shd->hts", queries, key_rows, preferred_element_type=jnp.float32)
    weights = (scores * decays).astype(jnp.bfloat16)
    intra_part = jnp.einsum("hts,shd->thd", weights, value_rows, preferred_element_type=jnp.float32)
    last_seg = seg_tok[tok_rows - 1]
    tail_gain = jnp.exp(
        jnp.where(
            (seg_tok == last_seg)[None, :], levels[:, tok_rows - 1 : tok_rows] - levels, NEG_FLOOR
        )
    )
    keyed = (key_rows * tail_gain.T[:, :, None]).astype(jnp.bfloat16)
    local_state = jnp.einsum("shd,she->hde", keyed, value_rows, preferred_element_type=jnp.float32)
    first_seg = seg_tok[0]
    joined = (first_seg == prev_last) & jnp.all(seg_tok == first_seg)
    carry_gain = jnp.where(joined, jnp.exp(levels[:, tok_rows - 1]), 0.0)
    reach_gain = jnp.where(
        ((seg_tok == first_seg) & (first_seg == prev_last))[None, :], jnp.exp(levels), 0.0
    )
    return (intra_part, (carry_gain, local_state), reach_gain, queries)


def absorb(running, queries, key_rows, value_rows, allowed):
    row_max, row_mass, weighted = running
    scores = jnp.einsum(
        "tkgd,skd->tkgs", queries, key_rows, preferred_element_type=jnp.float32
    ) * HEAD_DIM ** (-0.5)
    scores = jnp.where(allowed[:, None, None, :], scores, MASK_FILL)
    new_max = jnp.maximum(row_max, jnp.max(scores, axis=-1))
    exponent = jnp.exp(scores - new_max[..., None])
    shrink = jnp.exp(row_max - new_max)
    row_mass = row_mass * shrink + jnp.sum(exponent, axis=-1)
    update = jnp.einsum(
        "tkgs,skd->tkgd",
        exponent.astype(jnp.bfloat16),
        value_rows,
        preferred_element_type=jnp.float32,
    )
    weighted = weighted * shrink[..., None] + update
    return (new_max, row_mass, weighted)


def body(light_q, light_k, light_v, log_decay, light_gain, soft_q, soft_k, soft_v, segment_ids):
    tok_rows = light_q.shape[0]
    position = lax.axis_index(("grp", "seq"))
    row_start = position * tok_rows
    seg_tok = token_segments(segment_ids, row_start, tok_rows)
    prev_index = jnp.maximum(position * (tok_rows // BLOCK) - 1, 0)
    prev_last = jnp.where(
        position > 0, lax.dynamic_index_in_dim(segment_ids, prev_index, keepdims=False), -1
    )
    intra_part, element, reach_gain, queries = lightning_local(
        light_q, light_k, light_v, log_decay, seg_tok, prev_last
    )
    core = position % 2
    window_len = WINDOW_DEV
    kv_heads = soft_k.shape[1] // HEAD_DIM
    group_size = soft_q.shape[1] // soft_k.shape[1]
    soft_queries = soft_q.reshape(tok_rows, kv_heads, group_size, HEAD_DIM)
    query_pos = row_start + jnp.arange(tok_rows, dtype=jnp.int32)

    def take(running, slot_list, chosen):
        key_rows = chosen[:, 0].reshape(-1, kv_heads, HEAD_DIM)
        value_rows = chosen[:, 1].reshape(-1, kv_heads, HEAD_DIM)
        key_pos = jnp.concatenate(
            [
                (position - source) * tok_rows + jnp.arange(tok_rows, dtype=jnp.int32)
                for source in slot_list
            ]
        )
        key_seg = jnp.concatenate(
            [
                token_segments(segment_ids, jnp.maximum(position - source, 0) * tok_rows, tok_rows)
                for source in slot_list
            ]
        )
        allowed = (
            (key_pos[None, :] <= query_pos[:, None])
            & (key_pos >= 0)[None, :]
            & (key_seg[None, :] == seg_tok[:, None])
        )
        return absorb(running, soft_queries, key_rows, value_rows, allowed)

    running = (
        jnp.full((tok_rows, kv_heads, group_size), MASK_FILL, jnp.float32),
        jnp.zeros((tok_rows, kv_heads, group_size), jnp.float32),
        jnp.zeros((tok_rows, kv_heads, group_size, HEAD_DIM), jnp.float32),
    )
    state_rounded, running = exchange(
        element, jnp.stack([soft_k, soft_v]), ("grp", "seq"), core, window_len, take, running
    )
    inter_part = (
        jnp.einsum("thd,hde->the", queries, state_rounded, preferred_element_type=jnp.float32)
        * reach_gain.T[:, :, None]
    )
    mixed = (intra_part + inter_part).reshape(tok_rows, -1)
    square_sum = lax.psum(jnp.sum(mixed * mixed, axis=1), "head")
    inv_norm = lax.rsqrt(square_sum / (LIGHTNING_HEADS * HEAD_DIM) + 1e-06)
    light_out = (mixed * inv_norm[:, None] * light_gain).astype(jnp.bfloat16)
    row_max, row_mass, weighted = running
    soft_out = (weighted / row_mass[..., None]).reshape(tok_rows, -1).astype(jnp.bfloat16)
    return (light_out, soft_out)


def solution(mesh):
    placed = (
        P(("grp", "seq"), "head"),
        P(("grp", "seq"), "head"),
        P(("grp", "seq"), "head"),
        P("head", ("grp", "seq")),
        P("head"),
        P(("grp", "seq"), "head"),
        P(("grp", "seq"), "head"),
        P(("grp", "seq"), "head"),
        P(),
    )
    return jax.shard_map(
        body,
        mesh=mesh,
        in_specs=placed,
        out_specs=(P(("grp", "seq"), "head"), P(("grp", "seq"), "head")),
        check_vma=False,
    )
```

```python
import jax
import jax.numpy as jnp
from jax import lax
from jax.sharding import PartitionSpec as P

LIGHTNING_HEADS = 32
HEAD_DIM = 128
BLOCK = 128
WINDOW_DEV = 8


NEG_FLOOR = -10000.0
MASK_FILL = -1e30


def shift_pairs(count, by, parity=None):
    return [
        (i, i + by)
        for i in range(count)
        if 0 <= i + by < count and (parity is None or i % 2 == parity)
    ]


def exchange(element, kv_pair, axis, core, width, take, running):
    count = lax.axis_size(axis)
    half = width // 2
    swap = [(i, i ^ 1) for i in range(count)]
    ring = [kv_pair]

    def ring_step(parity=None):
        return lax.ppermute(ring[-1], axis, shift_pairs(count, 2, parity))

    gain, state = element
    rows = state.shape[1]
    packed = jnp.concatenate([state, jnp.broadcast_to(gain[:, None, None], state[:, :1].shape)], 1)
    got = lax.ppermute(packed, axis, shift_pairs(count, 1, 0))
    got, kv_next = lax.optimization_barrier((got, ring_step()))
    ring.append(kv_next)
    wide_state = got[:, :rows] * gain[:, None, None] + state
    wide_gain = got[:, rows, 0] * gain
    high = wide_gain.astype(jnp.bfloat16)
    low = (wide_gain - high.astype(jnp.float32)).astype(jnp.bfloat16)
    packed = jnp.concatenate(
        [
            wide_state.astype(jnp.bfloat16),
            jnp.broadcast_to(high[:, None, None], state[:, :1].shape),
            jnp.broadcast_to(low[:, None, None], state[:, :1].shape),
        ],
        1,
    )
    got = lax.ppermute(packed, axis, shift_pairs(count, 2, 1))
    got, kv_next = lax.optimization_barrier((got, ring_step()))
    ring.append(kv_next)
    got_gain = got[:, rows, 0].astype(jnp.float32) + got[:, rows + 1, 0].astype(jnp.float32)
    wide_state = got[:, :rows].astype(jnp.float32) * wide_gain[:, None, None] + wide_state
    wide_gain = got_gain * wide_gain
    got = lax.ppermute(wide_state.astype(jnp.bfloat16), axis, shift_pairs(count, 4, 1))
    got, kv_next = lax.optimization_barrier((got, ring_step()))
    ring.append(kv_next)
    wide_state = got.astype(jnp.float32) * wide_gain[:, None, None] + wide_state
    mine = jnp.stack(ring[:half])
    sent = jnp.where(core == 1, jnp.stack(ring[1:half]), jnp.stack(ring[: half - 1]))
    running = take(running, range(0, width, 2), mine)
    before = lax.ppermute(wide_state.astype(jnp.bfloat16), axis, shift_pairs(count, 1, 1))
    before, kv_next, theirs, running = lax.optimization_barrier(
        (before, ring_step(1), lax.ppermute(sent, axis, swap), running)
    )
    ring.append(kv_next)
    last = jnp.where(core == 1, ring[half], ring[half - 1])
    running = take(running, range(1, width - 2, 2), theirs)
    after = (before.astype(jnp.float32) * gain[:, None, None] + state).astype(jnp.bfloat16)
    after, last, running = lax.optimization_barrier(
        (
            lax.ppermute(after, axis, shift_pairs(count, 1, 0)),
            lax.ppermute(last, axis, swap),
            running,
        )
    )
    running = take(running, [width - 1], last[None])
    return jnp.where(core == 0, before, after), running


def lightning_local(light_q, light_k, light_v, log_decay, joined):
    tok_rows, feat_width = light_q.shape
    head_count = feat_width // HEAD_DIM
    queries = light_q.reshape(tok_rows, head_count, HEAD_DIM)
    key_rows = light_k.reshape(tok_rows, head_count, HEAD_DIM)
    value_rows = light_v.reshape(tok_rows, head_count, HEAD_DIM)
    levels = jnp.cumsum(log_decay, axis=1)
    offsets = jnp.arange(tok_rows, dtype=jnp.int32)
    allowed = offsets[:, None] >= offsets[None, :]
    decays = jnp.exp(jnp.where(allowed[None], levels[:, :, None] - levels[:, None, :], NEG_FLOOR))
    scores = jnp.einsum("thd,shd->hts", queries, key_rows, preferred_element_type=jnp.float32)
    weights = (scores * decays).astype(jnp.bfloat16)
    intra_part = jnp.einsum("hts,shd->thd", weights, value_rows, preferred_element_type=jnp.float32)
    tail_gain = jnp.exp(levels[:, tok_rows - 1 : tok_rows] - levels)
    keyed = (key_rows * tail_gain.T[:, :, None]).astype(jnp.bfloat16)
    local_state = jnp.einsum("shd,she->hde", keyed, value_rows, preferred_element_type=jnp.float32)
    carry_gain = jnp.where(joined, jnp.exp(levels[:, tok_rows - 1]), 0.0)
    reach_gain = jnp.where(joined, jnp.exp(levels), 0.0)
    return (intra_part, (carry_gain, local_state), reach_gain, queries)


def absorb(running, queries, key_rows, value_rows, allowed):
    row_max, row_mass, weighted = running
    scores = jnp.einsum(
        "tkgd,skd->tkgs", queries, key_rows, preferred_element_type=jnp.float32
    ) * HEAD_DIM ** (-0.5)
    scores = jnp.where(allowed[:, None, None, :], scores, MASK_FILL)
    new_max = jnp.maximum(row_max, jnp.max(scores, axis=-1))
    exponent = jnp.exp(scores - new_max[..., None])
    shrink = jnp.exp(row_max - new_max)
    row_mass = row_mass * shrink + jnp.sum(exponent, axis=-1)
    update = jnp.einsum(
        "tkgs,skd->tkgd",
        exponent.astype(jnp.bfloat16),
        value_rows,
        preferred_element_type=jnp.float32,
    )
    weighted = weighted * shrink[..., None] + update
    return (new_max, row_mass, weighted)


def body(light_q, light_k, light_v, log_decay, light_gain, soft_q, soft_k, soft_v, segment_ids):
    tok_rows = light_q.shape[0]
    assert tok_rows == BLOCK
    position = lax.axis_index(("grp", "seq"))
    here_seg = segment_ids[position]
    joined = (position > 0) & (segment_ids[jnp.maximum(position - 1, 0)] == here_seg)
    intra_part, element, reach_gain, queries = lightning_local(
        light_q, light_k, light_v, log_decay, joined
    )
    core = position % 2
    window_len = WINDOW_DEV
    kv_heads = soft_k.shape[1] // HEAD_DIM
    group_size = soft_q.shape[1] // soft_k.shape[1]
    soft_queries = soft_q.reshape(tok_rows, kv_heads, group_size, HEAD_DIM)

    causal = jnp.arange(tok_rows)[:, None] >= jnp.arange(tok_rows)[None, :]

    def take(running, slot_list, chosen):
        key_rows = chosen[:, 0].reshape(-1, kv_heads, HEAD_DIM)
        value_rows = chosen[:, 1].reshape(-1, kv_heads, HEAD_DIM)
        allowed = jnp.concatenate(
            [
                causal
                if source == 0
                else jnp.broadcast_to(
                    (position >= source)
                    & (segment_ids[jnp.maximum(position - source, 0)] == here_seg),
                    causal.shape,
                )
                for source in slot_list
            ],
            axis=1,
        )
        return absorb(running, soft_queries, key_rows, value_rows, allowed)

    running = (
        jnp.full((tok_rows, kv_heads, group_size), MASK_FILL, jnp.float32),
        jnp.zeros((tok_rows, kv_heads, group_size), jnp.float32),
        jnp.zeros((tok_rows, kv_heads, group_size, HEAD_DIM), jnp.float32),
    )
    state_rounded, running = exchange(
        element, jnp.stack([soft_k, soft_v]), ("grp", "seq"), core, window_len, take, running
    )
    inter_part = (
        jnp.einsum("thd,hde->the", queries, state_rounded, preferred_element_type=jnp.float32)
        * reach_gain.T[:, :, None]
    )
    mixed = (intra_part + inter_part).reshape(tok_rows, -1)
    square_sum = lax.psum(jnp.sum(mixed * mixed, axis=1), "head")
    inv_norm = lax.rsqrt(square_sum / (LIGHTNING_HEADS * HEAD_DIM) + 1e-06)
    light_out = (mixed * inv_norm[:, None] * light_gain).astype(jnp.bfloat16)
    row_max, row_mass, weighted = running
    soft_out = (weighted / row_mass[..., None]).reshape(tok_rows, -1).astype(jnp.bfloat16)
    return (light_out, soft_out)


def solution(mesh):
    placed = (
        P(("grp", "seq"), "head"),
        P(("grp", "seq"), "head"),
        P(("grp", "seq"), "head"),
        P("head", ("grp", "seq")),
        P("head"),
        P(("grp", "seq"), "head"),
        P(("grp", "seq"), "head"),
        P(("grp", "seq"), "head"),
        P(),
    )
    return jax.shard_map(
        body,
        mesh=mesh,
        in_specs=placed,
        out_specs=(P(("grp", "seq"), "head"), P(("grp", "seq"), "head")),
        check_vma=False,
    )
```

```python
import jax
import jax.numpy as jnp
from jax import lax
from jax.sharding import PartitionSpec as P

LIGHTNING_HEADS = 32
HEAD_DIM = 128
BLOCK = 128
WINDOW_DEV = 8


NEG_FLOOR = -10000.0
MASK_FILL = -1e30


def shift_pairs(count, by, parity=None):
    return [
        (i, i + by)
        for i in range(count)
        if 0 <= i + by < count and (parity is None or i % 2 == parity)
    ]


def exchange(element, kv_pair, axis, core, width, take, running):
    count = lax.axis_size(axis)
    half = width // 2
    swap = [(i, i ^ 1) for i in range(count)]
    ring = [kv_pair]

    def ring_step(parity=None):
        return lax.ppermute(ring[-1], axis, shift_pairs(count, 2, parity))

    gain, state = element
    rows = state.shape[1]
    packed = jnp.concatenate([state, jnp.broadcast_to(gain[:, None, None], state[:, :1].shape)], 1)
    got = lax.ppermute(packed, axis, shift_pairs(count, 1, 0))
    got, kv_next = lax.optimization_barrier((got, ring_step()))
    ring.append(kv_next)
    wide_state = got[:, :rows] * gain[:, None, None] + state
    wide_gain = got[:, rows, 0] * gain
    high = wide_gain.astype(jnp.bfloat16)
    low = (wide_gain - high.astype(jnp.float32)).astype(jnp.bfloat16)
    packed = jnp.concatenate(
        [
            wide_state.astype(jnp.bfloat16),
            jnp.broadcast_to(high[:, None, None], state[:, :1].shape),
            jnp.broadcast_to(low[:, None, None], state[:, :1].shape),
        ],
        1,
    )
    got = lax.ppermute(packed, axis, shift_pairs(count, 2, 1))
    got, kv_next = lax.optimization_barrier((got, ring_step()))
    ring.append(kv_next)
    got_gain = got[:, rows, 0].astype(jnp.float32) + got[:, rows + 1, 0].astype(jnp.float32)
    wide_state = got[:, :rows].astype(jnp.float32) * wide_gain[:, None, None] + wide_state
    wide_gain = got_gain * wide_gain
    got = lax.ppermute(wide_state.astype(jnp.bfloat16), axis, shift_pairs(count, 4, 1))
    got, kv_next = lax.optimization_barrier((got, ring_step()))
    ring.append(kv_next)
    wide_state = got.astype(jnp.float32) * wide_gain[:, None, None] + wide_state
    mine = jnp.stack(ring[:half])
    sent = jnp.where(core == 1, jnp.stack(ring[1:half]), jnp.stack(ring[: half - 1]))
    before = lax.ppermute(wide_state.astype(jnp.bfloat16), axis, shift_pairs(count, 1, 1))
    before, kv_next, theirs = lax.optimization_barrier(
        (before, ring_step(1), lax.ppermute(sent, axis, swap))
    )
    ring.append(kv_next)
    last = jnp.where(core == 1, ring[half], ring[half - 1])
    running = take(running, range(0, width, 2), mine)
    running = take(running, range(1, width - 2, 2), theirs)
    after = (before.astype(jnp.float32) * gain[:, None, None] + state).astype(jnp.bfloat16)
    after, last, running = lax.optimization_barrier(
        (
            lax.ppermute(after, axis, shift_pairs(count, 1, 0)),
            lax.ppermute(last, axis, swap),
            running,
        )
    )
    running = take(running, [width - 1], last[None])
    return jnp.where(core == 0, before, after), running


def lightning_local(light_q, light_k, light_v, log_decay, joined):
    tok_rows, feat_width = light_q.shape
    head_count = feat_width // HEAD_DIM
    queries = light_q.reshape(tok_rows, head_count, HEAD_DIM)
    key_rows = light_k.reshape(tok_rows, head_count, HEAD_DIM)
    value_rows = light_v.reshape(tok_rows, head_count, HEAD_DIM)
    levels = jnp.cumsum(log_decay, axis=1)
    offsets = jnp.arange(tok_rows, dtype=jnp.int32)
    allowed = offsets[:, None] >= offsets[None, :]
    decays = jnp.exp(jnp.where(allowed[None], levels[:, :, None] - levels[:, None, :], NEG_FLOOR))
    scores = jnp.einsum("thd,shd->hts", queries, key_rows, preferred_element_type=jnp.float32)
    weights = (scores * decays).astype(jnp.bfloat16)
    intra_part = jnp.einsum("hts,shd->thd", weights, value_rows, preferred_element_type=jnp.float32)
    tail_gain = jnp.exp(levels[:, tok_rows - 1 : tok_rows] - levels)
    keyed = (key_rows * tail_gain.T[:, :, None]).astype(jnp.bfloat16)
    local_state = jnp.einsum("shd,she->hde", keyed, value_rows, preferred_element_type=jnp.float32)
    carry_gain = jnp.where(joined, jnp.exp(levels[:, tok_rows - 1]), 0.0)
    reach_gain = jnp.where(joined, jnp.exp(levels), 0.0)
    return (intra_part, (carry_gain, local_state), reach_gain, queries)


def absorb(running, queries, key_rows, value_rows, allowed):
    row_max, row_mass, weighted = running
    scores = jnp.einsum(
        "tkgd,skd->tkgs", queries, key_rows, preferred_element_type=jnp.float32
    ) * HEAD_DIM ** (-0.5)
    scores = jnp.where(allowed[:, None, None, :], scores, MASK_FILL)
    new_max = jnp.maximum(row_max, jnp.max(scores, axis=-1))
    exponent = jnp.exp(scores - new_max[..., None])
    shrink = jnp.exp(row_max - new_max)
    row_mass = row_mass * shrink + jnp.sum(exponent, axis=-1)
    update = jnp.einsum(
        "tkgs,skd->tkgd",
        exponent.astype(jnp.bfloat16),
        value_rows,
        preferred_element_type=jnp.float32,
    )
    weighted = weighted * shrink[..., None] + update
    return (new_max, row_mass, weighted)


def body(light_q, light_k, light_v, log_decay, light_gain, soft_q, soft_k, soft_v, segment_ids):
    tok_rows = light_q.shape[0]
    assert tok_rows == BLOCK
    position = lax.axis_index(("grp", "seq"))
    here_seg = segment_ids[position]
    joined = (position > 0) & (segment_ids[jnp.maximum(position - 1, 0)] == here_seg)
    intra_part, element, reach_gain, queries = lightning_local(
        light_q, light_k, light_v, log_decay, joined
    )
    core = position % 2
    window_len = WINDOW_DEV
    kv_heads = soft_k.shape[1] // HEAD_DIM
    group_size = soft_q.shape[1] // soft_k.shape[1]
    soft_queries = soft_q.reshape(tok_rows, kv_heads, group_size, HEAD_DIM)

    causal = jnp.arange(tok_rows)[:, None] >= jnp.arange(tok_rows)[None, :]

    def take(running, slot_list, chosen):
        key_rows = chosen[:, 0].reshape(-1, kv_heads, HEAD_DIM)
        value_rows = chosen[:, 1].reshape(-1, kv_heads, HEAD_DIM)
        allowed = jnp.concatenate(
            [
                causal
                if source == 0
                else jnp.broadcast_to(
                    (position >= source)
                    & (segment_ids[jnp.maximum(position - source, 0)] == here_seg),
                    causal.shape,
                )
                for source in slot_list
            ],
            axis=1,
        )
        return absorb(running, soft_queries, key_rows, value_rows, allowed)

    running = (
        jnp.full((tok_rows, kv_heads, group_size), MASK_FILL, jnp.float32),
        jnp.zeros((tok_rows, kv_heads, group_size), jnp.float32),
        jnp.zeros((tok_rows, kv_heads, group_size, HEAD_DIM), jnp.float32),
    )
    state_rounded, running = exchange(
        element, jnp.stack([soft_k, soft_v]), ("grp", "seq"), core, window_len, take, running
    )
    inter_part = (
        jnp.einsum("thd,hde->the", queries, state_rounded, preferred_element_type=jnp.float32)
        * reach_gain.T[:, :, None]
    )
    mixed = (intra_part + inter_part).reshape(tok_rows, -1)
    square_sum = lax.psum(jnp.sum(mixed * mixed, axis=1), "head")
    inv_norm = lax.rsqrt(square_sum / (LIGHTNING_HEADS * HEAD_DIM) + 1e-06)
    light_out = (mixed * inv_norm[:, None] * light_gain).astype(jnp.bfloat16)
    row_max, row_mass, weighted = running
    soft_out = (weighted / row_mass[..., None]).reshape(tok_rows, -1).astype(jnp.bfloat16)
    return (light_out, soft_out)


def solution(mesh):
    placed = (
        P(("grp", "seq"), "head"),
        P(("grp", "seq"), "head"),
        P(("grp", "seq"), "head"),
        P("head", ("grp", "seq")),
        P("head"),
        P(("grp", "seq"), "head"),
        P(("grp", "seq"), "head"),
        P(("grp", "seq"), "head"),
        P(),
    )
    return jax.shard_map(
        body,
        mesh=mesh,
        in_specs=placed,
        out_specs=(P(("grp", "seq"), "head"), P(("grp", "seq"), "head")),
        check_vma=False,
    )
```

```python
import jax
import jax.numpy as jnp
from jax import lax
from jax.sharding import PartitionSpec as P


LIGHTNING_HEADS = 32
HEAD_DIM = 128
BLOCK = 128
WINDOW_DEV = 8


NEG_FLOOR = -10000.0
MASK_FILL = -1e30


def shift_pairs(count, by, parity=None):
    return [
        (i, i + by)
        for i in range(count)
        if 0 <= i + by < count and (parity is None or i % 2 == parity)
    ]


def exchange(element, kv_pair, axis, core, width, take, running):
    count = lax.axis_size(axis)
    half = width // 2
    swap = [(i, i ^ 1) for i in range(count)]
    ring = [kv_pair]

    def ring_step(parity=None):
        return lax.ppermute(ring[-1], axis, shift_pairs(count, 2, parity))

    gain, state = element
    rows = state.shape[1]
    packed = jnp.concatenate([state, jnp.broadcast_to(gain[:, None, None], state[:, :1].shape)], 1)
    kv_next = ring_step()
    got = lax.ppermute(packed, axis, shift_pairs(count, 1, 0))
    got, kv_next = lax.optimization_barrier((got, kv_next))
    ring.append(kv_next)
    wide_state = got[:, :rows] * gain[:, None, None] + state
    wide_gain = got[:, rows, 0] * gain
    high = wide_gain.astype(jnp.bfloat16)
    low = (wide_gain - high.astype(jnp.float32)).astype(jnp.bfloat16)
    packed = jnp.concatenate(
        [
            wide_state.astype(jnp.bfloat16),
            jnp.broadcast_to(high[:, None, None], state[:, :1].shape),
            jnp.broadcast_to(low[:, None, None], state[:, :1].shape),
        ],
        1,
    )
    got = lax.ppermute(packed, axis, shift_pairs(count, 2, 1))
    got, kv_next = lax.optimization_barrier((got, ring_step()))
    ring.append(kv_next)
    got_gain = got[:, rows, 0].astype(jnp.float32) + got[:, rows + 1, 0].astype(jnp.float32)
    wide_state = got[:, :rows].astype(jnp.float32) * wide_gain[:, None, None] + wide_state
    wide_gain = got_gain * wide_gain
    got = lax.ppermute(wide_state.astype(jnp.bfloat16), axis, shift_pairs(count, 4, 1))
    got, kv_next = lax.optimization_barrier((got, ring_step()))
    ring.append(kv_next)
    wide_state = got.astype(jnp.float32) * wide_gain[:, None, None] + wide_state
    mine = jnp.stack(ring[:half])
    sent = jnp.where(core == 1, jnp.stack(ring[1:half]), jnp.stack(ring[: half - 1]))
    before = lax.ppermute(wide_state.astype(jnp.bfloat16), axis, shift_pairs(count, 1, 1))
    before, kv_next, theirs = lax.optimization_barrier(
        (before, ring_step(1), lax.ppermute(sent, axis, swap))
    )
    ring.append(kv_next)
    last = jnp.where(core == 1, ring[half], ring[half - 1])
    running = take(running, range(0, width, 2), mine)
    running = take(running, range(1, width - 2, 2), theirs)
    after = (before.astype(jnp.float32) * gain[:, None, None] + state).astype(jnp.bfloat16)
    after, last, running = lax.optimization_barrier(
        (
            lax.ppermute(after, axis, shift_pairs(count, 1, 0)),
            lax.ppermute(last, axis, swap),
            running,
        )
    )
    running = take(running, [width - 1], last[None])
    return jnp.where(core == 0, before, after), running


def lightning_local(light_q, light_k, light_v, log_decay, joined):
    tok_rows, feat_width = light_q.shape
    head_count = feat_width // HEAD_DIM
    queries = light_q.reshape(tok_rows, head_count, HEAD_DIM)
    key_rows = light_k.reshape(tok_rows, head_count, HEAD_DIM)
    value_rows = light_v.reshape(tok_rows, head_count, HEAD_DIM)
    levels = jnp.cumsum(log_decay, axis=1)
    offsets = jnp.arange(tok_rows, dtype=jnp.int32)
    allowed = offsets[:, None] >= offsets[None, :]
    decays = jnp.exp(jnp.where(allowed[None], levels[:, :, None] - levels[:, None, :], NEG_FLOOR))
    scores = jnp.einsum("thd,shd->hts", queries, key_rows, preferred_element_type=jnp.float32)
    weights = (scores * decays).astype(jnp.bfloat16)
    intra_part = jnp.einsum("hts,shd->thd", weights, value_rows, preferred_element_type=jnp.float32)
    tail_gain = jnp.exp(levels[:, tok_rows - 1 : tok_rows] - levels)
    keyed = (key_rows * tail_gain.T[:, :, None]).astype(jnp.bfloat16)
    local_state = jnp.einsum("shd,she->hde", keyed, value_rows, preferred_element_type=jnp.float32)
    carry_gain = jnp.where(joined, jnp.exp(levels[:, tok_rows - 1]), 0.0)
    reach_gain = jnp.where(joined, jnp.exp(levels), 0.0)
    return (intra_part, (carry_gain, local_state), reach_gain, queries)


def absorb(running, queries, key_rows, value_rows, allowed):
    row_max, row_mass, weighted = running
    scores = jnp.einsum(
        "tkgd,skd->tkgs", queries, key_rows, preferred_element_type=jnp.float32
    ) * HEAD_DIM ** (-0.5)
    scores = jnp.where(allowed[:, None, None, :], scores, MASK_FILL)
    new_max = jnp.maximum(row_max, jnp.max(scores, axis=-1))
    exponent = jnp.exp(scores - new_max[..., None])
    shrink = jnp.exp(row_max - new_max)
    row_mass = row_mass * shrink + jnp.sum(exponent, axis=-1)
    update = jnp.einsum(
        "tkgs,skd->tkgd",
        exponent.astype(jnp.bfloat16),
        value_rows,
        preferred_element_type=jnp.float32,
    )
    weighted = weighted * shrink[..., None] + update
    return (new_max, row_mass, weighted)


def body(light_q, light_k, light_v, log_decay, light_gain, soft_q, soft_k, soft_v, segment_ids):
    tok_rows = light_q.shape[0]
    assert tok_rows == BLOCK
    position = lax.axis_index(("grp", "seq"))
    here_seg = segment_ids[position]
    joined = (position > 0) & (segment_ids[jnp.maximum(position - 1, 0)] == here_seg)
    intra_part, element, reach_gain, queries = lightning_local(
        light_q, light_k, light_v, log_decay, joined
    )
    core = position % 2
    window_len = WINDOW_DEV
    kv_heads = soft_k.shape[1] // HEAD_DIM
    group_size = soft_q.shape[1] // soft_k.shape[1]
    soft_queries = soft_q.reshape(tok_rows, kv_heads, group_size, HEAD_DIM)

    causal = jnp.arange(tok_rows)[:, None] >= jnp.arange(tok_rows)[None, :]

    def take(running, slot_list, chosen):
        key_rows = chosen[:, 0].reshape(-1, kv_heads, HEAD_DIM)
        value_rows = chosen[:, 1].reshape(-1, kv_heads, HEAD_DIM)
        allowed = jnp.concatenate(
            [
                causal
                if source == 0
                else jnp.broadcast_to(
                    (position >= source)
                    & (segment_ids[jnp.maximum(position - source, 0)] == here_seg),
                    causal.shape,
                )
                for source in slot_list
            ],
            axis=1,
        )
        return absorb(running, soft_queries, key_rows, value_rows, allowed)

    running = (
        jnp.full((tok_rows, kv_heads, group_size), MASK_FILL, jnp.float32),
        jnp.zeros((tok_rows, kv_heads, group_size), jnp.float32),
        jnp.zeros((tok_rows, kv_heads, group_size, HEAD_DIM), jnp.float32),
    )
    state_rounded, running = exchange(
        element, jnp.stack([soft_k, soft_v]), ("grp", "seq"), core, window_len, take, running
    )
    inter_part = (
        jnp.einsum("thd,hde->the", queries, state_rounded, preferred_element_type=jnp.float32)
        * reach_gain.T[:, :, None]
    )
    mixed = (intra_part + inter_part).reshape(tok_rows, -1)
    square_sum = lax.psum(jnp.sum(mixed * mixed, axis=1), "head")
    inv_norm = lax.rsqrt(square_sum / (LIGHTNING_HEADS * HEAD_DIM) + 1e-06)
    light_out = (mixed * inv_norm[:, None] * light_gain).astype(jnp.bfloat16)
    _, row_mass, weighted = running
    soft_out = (weighted / row_mass[..., None]).reshape(tok_rows, -1).astype(jnp.bfloat16)
    return (light_out, soft_out)


def solution(mesh):
    placed = (
        P(("grp", "seq"), "head"),
        P(("grp", "seq"), "head"),
        P(("grp", "seq"), "head"),
        P("head", ("grp", "seq")),
        P("head"),
        P(("grp", "seq"), "head"),
        P(("grp", "seq"), "head"),
        P(("grp", "seq"), "head"),
        P(),
    )

    return jax.shard_map(
        body,
        mesh=mesh,
        in_specs=placed,
        out_specs=(P(("grp", "seq"), "head"), P(("grp", "seq"), "head")),
        check_vma=False,
    )
```

```python
import jax
import jax.numpy as jnp
from jax import lax
from jax.sharding import PartitionSpec as P


LIGHTNING_HEADS = 32
HEAD_DIM = 128
BLOCK = 128


NEG_FLOOR = -10000.0
MASK_FILL = -1e30


def shift_pairs(count, by, parity=None):
    return [
        (i, i + by)
        for i in range(count)
        if 0 <= i + by < count and (parity is None or i % 2 == parity)
    ]


def exchange(element, kv_pair, axis, core, take, running):
    count = lax.axis_size(axis)
    swap = [(i, i ^ 1) for i in range(count)]
    ring = [kv_pair]

    def ring_step():
        return lax.ppermute(ring[-1], axis, shift_pairs(count, 2))

    gain, state = element
    rows = state.shape[1]
    row_of = lambda v: jnp.broadcast_to(v[:, None, None], state[:, :1].shape)
    packed = jnp.concatenate([state, row_of(gain)], 1)
    kv_next = ring_step()
    partner = lax.ppermute(packed, axis, shift_pairs(count, 1, 0))
    partner, kv_next = lax.optimization_barrier((partner, kv_next))
    ring.append(kv_next)
    partner_state, partner_gain = partner[:, :rows], partner[:, rows, 0]
    wide_state = partner_state * gain[:, None, None] + state
    wide_gain = partner_gain * gain
    high = wide_gain.astype(jnp.bfloat16)
    low = (wide_gain - high.astype(jnp.float32)).astype(jnp.bfloat16)
    packed = jnp.concatenate([wide_state.astype(jnp.bfloat16), row_of(high), row_of(low)], 1)
    got, kv_next = lax.optimization_barrier(
        (lax.ppermute(packed, axis, shift_pairs(count, 2, 1)), ring_step())
    )
    ring.append(kv_next)
    got_gain = got[:, rows, 0].astype(jnp.float32) + got[:, rows + 1, 0].astype(jnp.float32)
    wide_state = got[:, :rows].astype(jnp.float32) * wide_gain[:, None, None] + wide_state
    wide_gain = got_gain * wide_gain
    sent = jnp.where(core == 1, jnp.stack(ring[1:3]), jnp.stack(ring[0:2]))
    running = take(running, [0, 2], jnp.stack(ring[0:2]))
    got, kv_next, theirs, running = lax.optimization_barrier(
        (
            lax.ppermute(wide_state.astype(jnp.bfloat16), axis, shift_pairs(count, 4, 1)),
            ring_step(),
            lax.ppermute(sent, axis, swap),
            running,
        )
    )
    ring.append(kv_next)
    outgoing = (got.astype(jnp.float32) * wide_gain[:, None, None] + wide_state).astype(jnp.bfloat16)
    split = outgoing.size // HEAD_DIM
    cross = jnp.concatenate([outgoing.reshape(-1, HEAD_DIM), ring[3].reshape(-1, HEAD_DIM)])
    sent = jnp.where(core == 1, jnp.stack([ring[3], ring[3]]), jnp.stack(ring[2:4]))
    running = take(running, [4, 6, 1, 3], jnp.concatenate([jnp.stack(ring[2:4]), theirs]))
    cross, ahead, theirs, running = lax.optimization_barrier(
        (
            lax.ppermute(cross, axis, shift_pairs(count, 1, 1)),
            lax.ppermute(outgoing, axis, shift_pairs(count, 2, 1)),
            lax.ppermute(sent, axis, swap),
            running,
        )
    )
    behind = cross[:split].reshape(outgoing.shape)
    after = ahead.astype(jnp.float32) * partner_gain[:, None, None] + partner_state
    last = jnp.where(
        core == 0, jnp.stack([theirs[0], cross[split:].reshape(kv_pair.shape)]), theirs
    )
    running = take(running, [5, 7], last)
    return jnp.where(core == 0, behind, after.astype(jnp.bfloat16)), running


def lightning_local(light_q, light_k, light_v, log_decay, joined):
    tok_rows, feat_width = light_q.shape
    head_count = feat_width // HEAD_DIM
    queries = light_q.reshape(tok_rows, head_count, HEAD_DIM)
    key_rows = light_k.reshape(tok_rows, head_count, HEAD_DIM)
    value_rows = light_v.reshape(tok_rows, head_count, HEAD_DIM)
    levels = jnp.cumsum(log_decay, axis=1)
    offsets = jnp.arange(tok_rows, dtype=jnp.int32)
    allowed = offsets[:, None] >= offsets[None, :]
    decays = jnp.exp(jnp.where(allowed[None], levels[:, :, None] - levels[:, None, :], NEG_FLOOR))
    scores = jnp.einsum("thd,shd->hts", queries, key_rows, preferred_element_type=jnp.float32)
    weights = (scores * decays).astype(jnp.bfloat16)
    intra_part = jnp.einsum("hts,shd->thd", weights, value_rows, preferred_element_type=jnp.float32)
    tail_gain = jnp.exp(levels[:, tok_rows - 1 : tok_rows] - levels)
    keyed = (key_rows * tail_gain.T[:, :, None]).astype(jnp.bfloat16)
    local_state = jnp.einsum("shd,she->hde", keyed, value_rows, preferred_element_type=jnp.float32)
    carry_gain = jnp.where(joined, jnp.exp(levels[:, tok_rows - 1]), 0.0)
    reach_gain = jnp.where(joined, jnp.exp(levels), 0.0)
    return (intra_part, (carry_gain, local_state), reach_gain, queries)


def absorb(running, queries, key_rows, value_rows, allowed):
    row_max, row_mass, weighted = running
    scores = jnp.einsum(
        "tkgd,skd->tkgs", queries, key_rows, preferred_element_type=jnp.float32
    ) * HEAD_DIM ** (-0.5)
    scores = jnp.where(allowed[:, None, None, :], scores, MASK_FILL)
    new_max = jnp.maximum(row_max, jnp.max(scores, axis=-1))
    exponent = jnp.exp(scores - new_max[..., None])
    shrink = jnp.exp(row_max - new_max)
    row_mass = row_mass * shrink + jnp.sum(exponent, axis=-1)
    update = jnp.einsum(
        "tkgs,skd->tkgd",
        exponent.astype(jnp.bfloat16),
        value_rows,
        preferred_element_type=jnp.float32,
    )
    weighted = weighted * shrink[..., None] + update
    return (new_max, row_mass, weighted)


def body(light_q, light_k, light_v, log_decay, light_gain, soft_q, soft_k, soft_v, segment_ids):
    tok_rows = light_q.shape[0]
    assert tok_rows == BLOCK
    position = lax.axis_index(("grp", "seq"))
    here_seg = segment_ids[position]
    joined = (position > 0) & (segment_ids[jnp.maximum(position - 1, 0)] == here_seg)
    intra_part, element, reach_gain, queries = lightning_local(
        light_q, light_k, light_v, log_decay, joined
    )
    core = position % 2
    kv_heads = soft_k.shape[1] // HEAD_DIM
    group_size = soft_q.shape[1] // soft_k.shape[1]
    soft_queries = soft_q.reshape(tok_rows, kv_heads, group_size, HEAD_DIM)

    causal = jnp.arange(tok_rows)[:, None] >= jnp.arange(tok_rows)[None, :]

    def take(running, slot_list, chosen):
        key_rows = chosen[:, 0].reshape(-1, kv_heads, HEAD_DIM)
        value_rows = chosen[:, 1].reshape(-1, kv_heads, HEAD_DIM)
        allowed = jnp.concatenate(
            [
                causal
                if source == 0
                else jnp.broadcast_to(
                    (position >= source)
                    & (segment_ids[jnp.maximum(position - source, 0)] == here_seg),
                    causal.shape,
                )
                for source in slot_list
            ],
            axis=1,
        )
        return absorb(running, soft_queries, key_rows, value_rows, allowed)

    running = (
        jnp.full((tok_rows, kv_heads, group_size), MASK_FILL, jnp.float32),
        jnp.zeros((tok_rows, kv_heads, group_size), jnp.float32),
        jnp.zeros((tok_rows, kv_heads, group_size, HEAD_DIM), jnp.float32),
    )
    state_rounded, running = exchange(
        element, jnp.stack([soft_k, soft_v]), ("grp", "seq"), core, take, running
    )
    inter_part = (
        jnp.einsum("thd,hde->the", queries, state_rounded, preferred_element_type=jnp.float32)
        * reach_gain.T[:, :, None]
    )
    mixed = (intra_part + inter_part).reshape(tok_rows, -1)
    square_sum = lax.psum(jnp.sum(mixed * mixed, axis=1), "head")
    inv_norm = lax.rsqrt(square_sum / (LIGHTNING_HEADS * HEAD_DIM) + 1e-06)
    light_out = (mixed * inv_norm[:, None] * light_gain).astype(jnp.bfloat16)
    _, row_mass, weighted = running
    soft_out = (weighted / row_mass[..., None]).reshape(tok_rows, -1).astype(jnp.bfloat16)
    return (light_out, soft_out)


def solution(mesh):
    placed = (
        P(("grp", "seq"), "head"),
        P(("grp", "seq"), "head"),
        P(("grp", "seq"), "head"),
        P("head", ("grp", "seq")),
        P("head"),
        P(("grp", "seq"), "head"),
        P(("grp", "seq"), "head"),
        P(("grp", "seq"), "head"),
        P(),
    )

    return jax.shard_map(
        body,
        mesh=mesh,
        in_specs=placed,
        out_specs=(P(("grp", "seq"), "head"), P(("grp", "seq"), "head")),
        check_vma=False,
    )
```

```python
import jax
import jax.numpy as jnp
from jax import lax
from jax.sharding import PartitionSpec as P


LIGHTNING_HEADS = 32
HEAD_DIM = 128
BLOCK = 128
WINDOW_DEV = 8


NEG_FLOOR = -10000.0
MASK_FILL = -1e30


def shift_pairs(count, by, parity=None):
    return [
        (i, i + by)
        for i in range(count)
        if 0 <= i + by < count and (parity is None or i % 2 == parity)
    ]


def exchange(element, kv_pair, axis, core, width, take, running):
    count = lax.axis_size(axis)
    half = width // 2
    swap = [(i, i ^ 1) for i in range(count)]
    ring = [kv_pair]

    def ring_step(parity=None):
        return lax.ppermute(ring[-1], axis, shift_pairs(count, 2, parity))

    gain, state = element
    rows = state.shape[1]
    packed = jnp.concatenate([state, jnp.broadcast_to(gain[:, None, None], state[:, :1].shape)], 1)
    kv_next = ring_step()
    got = lax.ppermute(packed, axis, shift_pairs(count, 1, 0))
    got, kv_next = lax.optimization_barrier((got, kv_next))
    ring.append(kv_next)
    wide_state = got[:, :rows] * gain[:, None, None] + state
    wide_gain = got[:, rows, 0] * gain
    high = wide_gain.astype(jnp.bfloat16)
    low = (wide_gain - high.astype(jnp.float32)).astype(jnp.bfloat16)
    packed = jnp.concatenate(
        [
            wide_state.astype(jnp.bfloat16),
            jnp.broadcast_to(high[:, None, None], state[:, :1].shape),
            jnp.broadcast_to(low[:, None, None], state[:, :1].shape),
        ],
        1,
    )
    got = lax.ppermute(packed, axis, shift_pairs(count, 2, 1))
    got, kv_next = lax.optimization_barrier((got, ring_step()))
    ring.append(kv_next)
    got_gain = got[:, rows, 0].astype(jnp.float32) + got[:, rows + 1, 0].astype(jnp.float32)
    wide_state = got[:, :rows].astype(jnp.float32) * wide_gain[:, None, None] + wide_state
    wide_gain = got_gain * wide_gain
    got = lax.ppermute(wide_state.astype(jnp.bfloat16), axis, shift_pairs(count, 4, 1))
    got, kv_next = lax.optimization_barrier((got, ring_step()))
    ring.append(kv_next)
    wide_state = got.astype(jnp.float32) * wide_gain[:, None, None] + wide_state
    mine = jnp.stack(ring[:half])
    sent = jnp.where(core == 1, jnp.stack(ring[1:half]), jnp.stack(ring[: half - 1]))
    before = lax.ppermute(wide_state.astype(jnp.bfloat16), axis, shift_pairs(count, 1, 1))
    before, kv_next, theirs = lax.optimization_barrier(
        (before, ring_step(1), lax.ppermute(sent, axis, swap))
    )
    ring.append(kv_next)
    last = jnp.where(core == 1, ring[half], ring[half - 1])
    running = take(running, range(0, width, 2), mine)
    running = take(running, range(1, width - 2, 2), theirs)
    after = (before.astype(jnp.float32) * gain[:, None, None] + state).astype(jnp.bfloat16)
    split = after.size // HEAD_DIM
    both = jnp.concatenate([after.reshape(-1, HEAD_DIM), last.reshape(-1, HEAD_DIM)])
    both, running = lax.optimization_barrier((lax.ppermute(both, axis, swap), running))
    after = both[:split].reshape(after.shape)
    last = both[split:].reshape(last.shape)
    running = take(running, [width - 1], last[None])
    return jnp.where(core == 0, before, after), running


def lightning_local(light_q, light_k, light_v, log_decay, joined):
    tok_rows, feat_width = light_q.shape
    head_count = feat_width // HEAD_DIM
    queries = light_q.reshape(tok_rows, head_count, HEAD_DIM)
    key_rows = light_k.reshape(tok_rows, head_count, HEAD_DIM)
    value_rows = light_v.reshape(tok_rows, head_count, HEAD_DIM)
    levels = jnp.cumsum(log_decay, axis=1)
    offsets = jnp.arange(tok_rows, dtype=jnp.int32)
    allowed = offsets[:, None] >= offsets[None, :]
    decays = jnp.exp(jnp.where(allowed[None], levels[:, :, None] - levels[:, None, :], NEG_FLOOR))
    scores = jnp.einsum("thd,shd->hts", queries, key_rows, preferred_element_type=jnp.float32)
    weights = (scores * decays).astype(jnp.bfloat16)
    intra_part = jnp.einsum("hts,shd->thd", weights, value_rows, preferred_element_type=jnp.float32)
    tail_gain = jnp.exp(levels[:, tok_rows - 1 : tok_rows] - levels)
    keyed = (key_rows * tail_gain.T[:, :, None]).astype(jnp.bfloat16)
    local_state = jnp.einsum("shd,she->hde", keyed, value_rows, preferred_element_type=jnp.float32)
    carry_gain = jnp.where(joined, jnp.exp(levels[:, tok_rows - 1]), 0.0)
    reach_gain = jnp.where(joined, jnp.exp(levels), 0.0)
    return (intra_part, (carry_gain, local_state), reach_gain, queries)


def absorb(running, queries, key_rows, value_rows, allowed):
    row_max, row_mass, weighted = running
    scores = jnp.einsum(
        "tkgd,skd->tkgs", queries, key_rows, preferred_element_type=jnp.float32
    ) * HEAD_DIM ** (-0.5)
    scores = jnp.where(allowed[:, None, None, :], scores, MASK_FILL)
    new_max = jnp.maximum(row_max, jnp.max(scores, axis=-1))
    exponent = jnp.exp(scores - new_max[..., None])
    shrink = jnp.exp(row_max - new_max)
    row_mass = row_mass * shrink + jnp.sum(exponent, axis=-1)
    update = jnp.einsum(
        "tkgs,skd->tkgd",
        exponent.astype(jnp.bfloat16),
        value_rows,
        preferred_element_type=jnp.float32,
    )
    weighted = weighted * shrink[..., None] + update
    return (new_max, row_mass, weighted)


def body(light_q, light_k, light_v, log_decay, light_gain, soft_q, soft_k, soft_v, segment_ids):
    tok_rows = light_q.shape[0]
    assert tok_rows == BLOCK
    position = lax.axis_index(("grp", "seq"))
    here_seg = segment_ids[position]
    joined = (position > 0) & (segment_ids[jnp.maximum(position - 1, 0)] == here_seg)
    intra_part, element, reach_gain, queries = lightning_local(
        light_q, light_k, light_v, log_decay, joined
    )
    core = position % 2
    window_len = WINDOW_DEV
    kv_heads = soft_k.shape[1] // HEAD_DIM
    group_size = soft_q.shape[1] // soft_k.shape[1]
    soft_queries = soft_q.reshape(tok_rows, kv_heads, group_size, HEAD_DIM)

    causal = jnp.arange(tok_rows)[:, None] >= jnp.arange(tok_rows)[None, :]

    def take(running, slot_list, chosen):
        key_rows = chosen[:, 0].reshape(-1, kv_heads, HEAD_DIM)
        value_rows = chosen[:, 1].reshape(-1, kv_heads, HEAD_DIM)
        allowed = jnp.concatenate(
            [
                causal
                if source == 0
                else jnp.broadcast_to(
                    (position >= source)
                    & (segment_ids[jnp.maximum(position - source, 0)] == here_seg),
                    causal.shape,
                )
                for source in slot_list
            ],
            axis=1,
        )
        return absorb(running, soft_queries, key_rows, value_rows, allowed)

    running = (
        jnp.full((tok_rows, kv_heads, group_size), MASK_FILL, jnp.float32),
        jnp.zeros((tok_rows, kv_heads, group_size), jnp.float32),
        jnp.zeros((tok_rows, kv_heads, group_size, HEAD_DIM), jnp.float32),
    )
    state_rounded, running = exchange(
        element, jnp.stack([soft_k, soft_v]), ("grp", "seq"), core, window_len, take, running
    )
    inter_part = (
        jnp.einsum("thd,hde->the", queries, state_rounded, preferred_element_type=jnp.float32)
        * reach_gain.T[:, :, None]
    )
    mixed = (intra_part + inter_part).reshape(tok_rows, -1)
    square_sum = lax.psum(jnp.sum(mixed * mixed, axis=1), "head")
    inv_norm = lax.rsqrt(square_sum / (LIGHTNING_HEADS * HEAD_DIM) + 1e-06)
    light_out = (mixed * inv_norm[:, None] * light_gain).astype(jnp.bfloat16)
    _, row_mass, weighted = running
    soft_out = (weighted / row_mass[..., None]).reshape(tok_rows, -1).astype(jnp.bfloat16)
    return (light_out, soft_out)


def solution(mesh):
    placed = (
        P(("grp", "seq"), "head"),
        P(("grp", "seq"), "head"),
        P(("grp", "seq"), "head"),
        P("head", ("grp", "seq")),
        P("head"),
        P(("grp", "seq"), "head"),
        P(("grp", "seq"), "head"),
        P(("grp", "seq"), "head"),
        P(),
    )

    return jax.shard_map(
        body,
        mesh=mesh,
        in_specs=placed,
        out_specs=(P(("grp", "seq"), "head"), P(("grp", "seq"), "head")),
        check_vma=False,
    )
```

```python
import jax
import jax.numpy as jnp
from jax import lax
from jax.sharding import PartitionSpec as P


LIGHTNING_HEADS = 32
HEAD_DIM = 128
BLOCK = 128
WINDOW_DEV = 8


NEG_FLOOR = -10000.0
MASK_FILL = -1e30


def shift_pairs(count, by, parity=None):
    return [
        (i, i + by)
        for i in range(count)
        if 0 <= i + by < count and (parity is None or i % 2 == parity)
    ]


def exchange(element, kv_pair, axis, core, width, take, running):
    count = lax.axis_size(axis)
    half = width // 2
    swap = [(i, i ^ 1) for i in range(count)]
    ring = [kv_pair]

    def ring_step(parity=None):
        return lax.ppermute(ring[-1], axis, shift_pairs(count, 2, parity))

    gain, state = element
    rows = state.shape[1]
    packed = jnp.concatenate([state, jnp.broadcast_to(gain[:, None, None], state[:, :1].shape)], 1)
    kv_next = ring_step()
    got = lax.ppermute(packed, axis, shift_pairs(count, 1, 0))
    got, kv_next = lax.optimization_barrier((got, kv_next))
    ring.append(kv_next)
    wide_state = got[:, :rows] * gain[:, None, None] + state
    wide_gain = got[:, rows, 0] * gain
    high = wide_gain.astype(jnp.bfloat16)
    low = (wide_gain - high.astype(jnp.float32)).astype(jnp.bfloat16)
    packed = jnp.concatenate(
        [
            wide_state.astype(jnp.bfloat16),
            jnp.broadcast_to(high[:, None, None], state[:, :1].shape),
            jnp.broadcast_to(low[:, None, None], state[:, :1].shape),
        ],
        1,
    )
    got = lax.ppermute(packed, axis, shift_pairs(count, 2, 1))
    got, kv_next = lax.optimization_barrier((got, ring_step()))
    ring.append(kv_next)
    got_gain = got[:, rows, 0].astype(jnp.float32) + got[:, rows + 1, 0].astype(jnp.float32)
    wide_state = got[:, :rows].astype(jnp.float32) * wide_gain[:, None, None] + wide_state
    wide_gain = got_gain * wide_gain
    got = lax.ppermute(wide_state.astype(jnp.bfloat16), axis, shift_pairs(count, 4, 1))
    got, kv_next = lax.optimization_barrier((got, ring_step()))
    ring.append(kv_next)
    wide_state = got.astype(jnp.float32) * wide_gain[:, None, None] + wide_state
    mine = jnp.stack(ring[:half])
    sent = jnp.where(core == 1, jnp.stack(ring[1:half]), jnp.stack(ring[: half - 1]))
    before = lax.ppermute(wide_state.astype(jnp.bfloat16), axis, shift_pairs(count, 1, 1))
    before, kv_next, theirs = lax.optimization_barrier(
        (before, ring_step(1), lax.ppermute(sent, axis, swap))
    )
    ring.append(kv_next)
    last = jnp.where(core == 1, ring[half], ring[half - 1])
    running = take(running, range(0, width, 2), mine)
    running = take(running, range(1, width - 2, 2), theirs)
    after = (before.astype(jnp.float32) * gain[:, None, None] + state).astype(jnp.bfloat16)
    after, last, running = lax.optimization_barrier(
        (
            lax.ppermute(after, axis, shift_pairs(count, 1, 0)),
            lax.ppermute(last, axis, swap),
            running,
        )
    )
    running = take(running, [width - 1], last[None])
    return jnp.where(core == 0, before, after), running


def butterfly_sum(x, axis):
    count = lax.axis_size(axis)
    step = 1
    while step < count:
        x = x + lax.ppermute(x, axis, [(i, i ^ step) for i in range(count)])
        step *= 2
    return x


def lightning_local(light_q, light_k, light_v, log_decay, joined):
    tok_rows, feat_width = light_q.shape
    head_count = feat_width // HEAD_DIM
    queries = light_q.reshape(tok_rows, head_count, HEAD_DIM)
    key_rows = light_k.reshape(tok_rows, head_count, HEAD_DIM)
    value_rows = light_v.reshape(tok_rows, head_count, HEAD_DIM)
    levels = jnp.cumsum(log_decay, axis=1)
    offsets = jnp.arange(tok_rows, dtype=jnp.int32)
    allowed = offsets[:, None] >= offsets[None, :]
    decays = jnp.exp(jnp.where(allowed[None], levels[:, :, None] - levels[:, None, :], NEG_FLOOR))
    scores = jnp.einsum("thd,shd->hts", queries, key_rows, preferred_element_type=jnp.float32)
    weights = (scores * decays).astype(jnp.bfloat16)
    intra_part = jnp.einsum("hts,shd->thd", weights, value_rows, preferred_element_type=jnp.float32)
    tail_gain = jnp.exp(levels[:, tok_rows - 1 : tok_rows] - levels)
    keyed = (key_rows * tail_gain.T[:, :, None]).astype(jnp.bfloat16)
    local_state = jnp.einsum("shd,she->hde", keyed, value_rows, preferred_element_type=jnp.float32)
    carry_gain = jnp.where(joined, jnp.exp(levels[:, tok_rows - 1]), 0.0)
    reach_gain = jnp.where(joined, jnp.exp(levels), 0.0)
    return (intra_part, (carry_gain, local_state), reach_gain, queries)


def absorb(running, queries, key_rows, value_rows, allowed):
    row_max, row_mass, weighted = running
    scores = jnp.einsum(
        "tkgd,skd->tkgs", queries, key_rows, preferred_element_type=jnp.float32
    ) * HEAD_DIM ** (-0.5)
    scores = jnp.where(allowed[:, None, None, :], scores, MASK_FILL)
    new_max = jnp.maximum(row_max, jnp.max(scores, axis=-1))
    exponent = jnp.exp(scores - new_max[..., None])
    shrink = jnp.exp(row_max - new_max)
    row_mass = row_mass * shrink + jnp.sum(exponent, axis=-1)
    update = jnp.einsum(
        "tkgs,skd->tkgd",
        exponent.astype(jnp.bfloat16),
        value_rows,
        preferred_element_type=jnp.float32,
    )
    weighted = weighted * shrink[..., None] + update
    return (new_max, row_mass, weighted)


def body(light_q, light_k, light_v, log_decay, light_gain, soft_q, soft_k, soft_v, segment_ids):
    tok_rows = light_q.shape[0]
    assert tok_rows == BLOCK
    position = lax.axis_index(("grp", "seq"))
    here_seg = segment_ids[position]
    joined = (position > 0) & (segment_ids[jnp.maximum(position - 1, 0)] == here_seg)
    intra_part, element, reach_gain, queries = lightning_local(
        light_q, light_k, light_v, log_decay, joined
    )
    core = position % 2
    window_len = WINDOW_DEV
    kv_heads = soft_k.shape[1] // HEAD_DIM
    group_size = soft_q.shape[1] // soft_k.shape[1]
    soft_queries = soft_q.reshape(tok_rows, kv_heads, group_size, HEAD_DIM)

    causal = jnp.arange(tok_rows)[:, None] >= jnp.arange(tok_rows)[None, :]

    def take(running, slot_list, chosen):
        key_rows = chosen[:, 0].reshape(-1, kv_heads, HEAD_DIM)
        value_rows = chosen[:, 1].reshape(-1, kv_heads, HEAD_DIM)
        allowed = jnp.concatenate(
            [
                causal
                if source == 0
                else jnp.broadcast_to(
                    (position >= source)
                    & (segment_ids[jnp.maximum(position - source, 0)] == here_seg),
                    causal.shape,
                )
                for source in slot_list
            ],
            axis=1,
        )
        return absorb(running, soft_queries, key_rows, value_rows, allowed)

    running = (
        jnp.full((tok_rows, kv_heads, group_size), MASK_FILL, jnp.float32),
        jnp.zeros((tok_rows, kv_heads, group_size), jnp.float32),
        jnp.zeros((tok_rows, kv_heads, group_size, HEAD_DIM), jnp.float32),
    )
    state_rounded, running = exchange(
        element, jnp.stack([soft_k, soft_v]), ("grp", "seq"), core, window_len, take, running
    )
    inter_part = (
        jnp.einsum("thd,hde->the", queries, state_rounded, preferred_element_type=jnp.float32)
        * reach_gain.T[:, :, None]
    )
    mixed = (intra_part + inter_part).reshape(tok_rows, -1)
    square_sum = butterfly_sum(jnp.sum(mixed * mixed, axis=1), "head")
    inv_norm = lax.rsqrt(square_sum / (LIGHTNING_HEADS * HEAD_DIM) + 1e-06)
    light_out = (mixed * inv_norm[:, None] * light_gain).astype(jnp.bfloat16)
    _, row_mass, weighted = running
    soft_out = (weighted / row_mass[..., None]).reshape(tok_rows, -1).astype(jnp.bfloat16)
    return (light_out, soft_out)


def solution(mesh):
    placed = (
        P(("grp", "seq"), "head"),
        P(("grp", "seq"), "head"),
        P(("grp", "seq"), "head"),
        P("head", ("grp", "seq")),
        P("head"),
        P(("grp", "seq"), "head"),
        P(("grp", "seq"), "head"),
        P(("grp", "seq"), "head"),
        P(),
    )

    return jax.shard_map(
        body,
        mesh=mesh,
        in_specs=placed,
        out_specs=(P(("grp", "seq"), "head"), P(("grp", "seq"), "head")),
        check_vma=False,
    )
```

```python
import jax
import jax.numpy as jnp
from jax import lax
from jax.sharding import PartitionSpec as P


LIGHTNING_HEADS = 32
HEAD_DIM = 128
BLOCK = 128
WINDOW_DEV = 8


NEG_FLOOR = -10000.0
MASK_FILL = -1e30


def shift_pairs(count, by, parity=None):
    return [
        (i, i + by)
        for i in range(count)
        if 0 <= i + by < count and (parity is None or i % 2 == parity)
    ]


def exchange(element, kv_pair, axis, core, width, take, running):
    count = lax.axis_size(axis)
    half = width // 2
    swap = [(i, i ^ 1) for i in range(count)]
    ring = [kv_pair]

    def ring_step(parity=None):
        return lax.ppermute(ring[-1], axis, shift_pairs(count, 2, parity))

    gain, state = element
    rows = state.shape[1]
    packed = jnp.concatenate([state, jnp.broadcast_to(gain[:, None, None], state[:, :1].shape)], 1)
    kv_next = ring_step()
    got = lax.ppermute(packed, axis, shift_pairs(count, 1, 0))
    got, kv_next = lax.optimization_barrier((got, kv_next))
    ring.append(kv_next)
    wide_state = got[:, :rows] * gain[:, None, None] + state
    wide_gain = got[:, rows, 0] * gain
    high = wide_gain.astype(jnp.bfloat16)
    low = (wide_gain - high.astype(jnp.float32)).astype(jnp.bfloat16)
    packed = jnp.concatenate(
        [
            wide_state.astype(jnp.bfloat16),
            jnp.broadcast_to(high[:, None, None], state[:, :1].shape),
            jnp.broadcast_to(low[:, None, None], state[:, :1].shape),
        ],
        1,
    )
    got = lax.ppermute(packed, axis, shift_pairs(count, 2, 1))
    got, kv_next = lax.optimization_barrier((got, ring_step()))
    ring.append(kv_next)
    got_gain = got[:, rows, 0].astype(jnp.float32) + got[:, rows + 1, 0].astype(jnp.float32)
    wide_state = got[:, :rows].astype(jnp.float32) * wide_gain[:, None, None] + wide_state
    wide_gain = got_gain * wide_gain
    got = lax.ppermute(wide_state.astype(jnp.bfloat16), axis, shift_pairs(count, 4, 1))
    kv_next = ring_step()
    got, kv_next = lax.optimization_barrier((got, kv_next))
    ring.append(kv_next)
    wide_state = got.astype(jnp.float32) * wide_gain[:, None, None] + wide_state
    mine = jnp.stack(ring[:half])
    sent = jnp.where(core == 1, jnp.stack(ring[1:half]), jnp.stack(ring[: half - 1]))
    before = lax.ppermute(wide_state.astype(jnp.bfloat16), axis, shift_pairs(count, 1, 1))
    kv_next = ring_step(1)
    theirs = lax.ppermute(sent, axis, swap)
    running = take(running, range(0, width, 2), mine)
    before, kv_next, theirs, running = lax.optimization_barrier((before, kv_next, theirs, running))
    ring.append(kv_next)
    last = jnp.where(core == 1, ring[half], ring[half - 1])
    running = take(running, range(1, width - 2, 2), theirs)
    after = (before.astype(jnp.float32) * gain[:, None, None] + state).astype(jnp.bfloat16)
    after = lax.ppermute(after, axis, shift_pairs(count, 1, 0))
    last = lax.ppermute(last, axis, swap)
    after, last, running = lax.optimization_barrier((after, last, running))
    running = take(running, [width - 1], last[None])
    return jnp.where(core == 0, before, after), running


def butterfly_sum(x, axis):
    count = lax.axis_size(axis)
    step = 1
    while step < count:
        x = x + lax.ppermute(x, axis, [(i, i ^ step) for i in range(count)])
        step *= 2
    return x


def lightning_local(light_q, light_k, light_v, log_decay, joined):
    tok_rows, feat_width = light_q.shape
    head_count = feat_width // HEAD_DIM
    queries = light_q.reshape(tok_rows, head_count, HEAD_DIM)
    key_rows = light_k.reshape(tok_rows, head_count, HEAD_DIM)
    value_rows = light_v.reshape(tok_rows, head_count, HEAD_DIM)
    levels = jnp.cumsum(log_decay, axis=1)
    offsets = jnp.arange(tok_rows, dtype=jnp.int32)
    allowed = offsets[:, None] >= offsets[None, :]
    decays = jnp.exp(jnp.where(allowed[None], levels[:, :, None] - levels[:, None, :], NEG_FLOOR))
    scores = jnp.einsum("thd,shd->hts", queries, key_rows, preferred_element_type=jnp.float32)
    weights = (scores * decays).astype(jnp.bfloat16)
    intra_part = jnp.einsum("hts,shd->thd", weights, value_rows, preferred_element_type=jnp.float32)
    tail_gain = jnp.exp(levels[:, tok_rows - 1 : tok_rows] - levels)
    keyed = (key_rows * tail_gain.T[:, :, None]).astype(jnp.bfloat16)
    local_state = jnp.einsum("shd,she->hde", keyed, value_rows, preferred_element_type=jnp.float32)
    carry_gain = jnp.where(joined, jnp.exp(levels[:, tok_rows - 1]), 0.0)
    reach_gain = jnp.where(joined, jnp.exp(levels), 0.0)
    return (intra_part, (carry_gain, local_state), reach_gain, queries)


def absorb(running, queries, key_rows, value_rows, allowed):
    row_max, row_mass, weighted = running
    scores = jnp.einsum(
        "tkgd,skd->tkgs", queries, key_rows, preferred_element_type=jnp.float32
    ) * HEAD_DIM ** (-0.5)
    scores = jnp.where(allowed[:, None, None, :], scores, MASK_FILL)
    new_max = jnp.maximum(row_max, jnp.max(scores, axis=-1))
    exponent = jnp.exp(scores - new_max[..., None])
    shrink = jnp.exp(row_max - new_max)
    row_mass = row_mass * shrink + jnp.sum(exponent, axis=-1)
    update = jnp.einsum(
        "tkgs,skd->tkgd",
        exponent.astype(jnp.bfloat16),
        value_rows,
        preferred_element_type=jnp.float32,
    )
    weighted = weighted * shrink[..., None] + update
    return (new_max, row_mass, weighted)


def body(light_q, light_k, light_v, log_decay, light_gain, soft_q, soft_k, soft_v, segment_ids):
    tok_rows = light_q.shape[0]
    assert tok_rows == BLOCK
    position = lax.axis_index(("grp", "seq"))
    here_seg = segment_ids[position]
    joined = (position > 0) & (segment_ids[jnp.maximum(position - 1, 0)] == here_seg)
    intra_part, element, reach_gain, queries = lightning_local(
        light_q, light_k, light_v, log_decay, joined
    )
    core = position % 2
    window_len = WINDOW_DEV
    kv_heads = soft_k.shape[1] // HEAD_DIM
    group_size = soft_q.shape[1] // soft_k.shape[1]
    soft_queries = soft_q.reshape(tok_rows, kv_heads, group_size, HEAD_DIM)

    causal = jnp.arange(tok_rows)[:, None] >= jnp.arange(tok_rows)[None, :]

    def take(running, slot_list, chosen):
        key_rows = chosen[:, 0].reshape(-1, kv_heads, HEAD_DIM)
        value_rows = chosen[:, 1].reshape(-1, kv_heads, HEAD_DIM)
        allowed = jnp.concatenate(
            [
                causal
                if source == 0
                else jnp.broadcast_to(
                    (position >= source)
                    & (segment_ids[jnp.maximum(position - source, 0)] == here_seg),
                    causal.shape,
                )
                for source in slot_list
            ],
            axis=1,
        )
        return absorb(running, soft_queries, key_rows, value_rows, allowed)

    running = (
        jnp.full((tok_rows, kv_heads, group_size), MASK_FILL, jnp.float32),
        jnp.zeros((tok_rows, kv_heads, group_size), jnp.float32),
        jnp.zeros((tok_rows, kv_heads, group_size, HEAD_DIM), jnp.float32),
    )
    state_rounded, running = exchange(
        element, jnp.stack([soft_k, soft_v]), ("grp", "seq"), core, window_len, take, running
    )
    inter_part = (
        jnp.einsum("thd,hde->the", queries, state_rounded, preferred_element_type=jnp.float32)
        * reach_gain.T[:, :, None]
    )
    mixed = (intra_part + inter_part).reshape(tok_rows, -1)
    square_sum = butterfly_sum(jnp.sum(mixed * mixed, axis=1), "head")
    inv_norm = lax.rsqrt(square_sum / (LIGHTNING_HEADS * HEAD_DIM) + 1e-06)
    light_out = (mixed * inv_norm[:, None] * light_gain).astype(jnp.bfloat16)
    _, row_mass, weighted = running
    soft_out = (weighted / row_mass[..., None]).reshape(tok_rows, -1).astype(jnp.bfloat16)
    return (light_out, soft_out)


def solution(mesh):
    placed = (
        P(("grp", "seq"), "head"),
        P(("grp", "seq"), "head"),
        P(("grp", "seq"), "head"),
        P("head", ("grp", "seq")),
        P("head"),
        P(("grp", "seq"), "head"),
        P(("grp", "seq"), "head"),
        P(("grp", "seq"), "head"),
        P(),
    )

    return jax.shard_map(
        body,
        mesh=mesh,
        in_specs=placed,
        out_specs=(P(("grp", "seq"), "head"), P(("grp", "seq"), "head")),
        check_vma=False,
    )
```

```python
import jax
import jax.numpy as jnp
from jax import lax
from jax.sharding import PartitionSpec as P


LIGHTNING_HEADS = 32
HEAD_DIM = 128
BLOCK = 128
WINDOW_DEV = 8


NEG_FLOOR = -10000.0
MASK_FILL = -1e30


def shift_pairs(count, by, parity=None):
    return [
        (i, i + by)
        for i in range(count)
        if 0 <= i + by < count and (parity is None or i % 2 == parity)
    ]


def exchange(element, kv_pair, axis, core, width, take, running):
    count = lax.axis_size(axis)
    half = width // 2
    swap = [(i, i ^ 1) for i in range(count)]
    ring = [kv_pair]

    def ring_step(parity=None):
        return lax.ppermute(ring[-1], axis, shift_pairs(count, 2, parity))

    gain, state = element
    rows = state.shape[1]
    packed = jnp.concatenate([state, jnp.broadcast_to(gain[:, None, None], state[:, :1].shape)], 1)
    kv_next = ring_step()
    got = lax.ppermute(packed, axis, shift_pairs(count, 1, 0))
    got, kv_next = lax.optimization_barrier((got, kv_next))
    ring.append(kv_next)
    wide_state = got[:, :rows] * gain[:, None, None] + state
    wide_gain = got[:, rows, 0] * gain
    high = wide_gain.astype(jnp.bfloat16)
    low = (wide_gain - high.astype(jnp.float32)).astype(jnp.bfloat16)
    packed = jnp.concatenate(
        [
            wide_state.astype(jnp.bfloat16),
            jnp.broadcast_to(high[:, None, None], state[:, :1].shape),
            jnp.broadcast_to(low[:, None, None], state[:, :1].shape),
        ],
        1,
    )
    got = lax.ppermute(packed, axis, shift_pairs(count, 2, 1))
    got, kv_next = lax.optimization_barrier((got, ring_step()))
    ring.append(kv_next)
    got_gain = got[:, rows, 0].astype(jnp.float32) + got[:, rows + 1, 0].astype(jnp.float32)
    wide_state = got[:, :rows].astype(jnp.float32) * wide_gain[:, None, None] + wide_state
    wide_gain = got_gain * wide_gain
    got = lax.ppermute(wide_state.astype(jnp.bfloat16), axis, shift_pairs(count, 4, 1))
    kv_next = ring_step()
    got, kv_next = lax.optimization_barrier((got, kv_next))
    ring.append(kv_next)
    wide_state = got.astype(jnp.float32) * wide_gain[:, None, None] + wide_state
    mine = jnp.stack(ring[:half])
    sent = jnp.where(core == 1, jnp.stack(ring[1:half]), jnp.stack(ring[: half - 1]))
    before = lax.ppermute(wide_state.astype(jnp.bfloat16), axis, shift_pairs(count, 1, 1))
    kv_next = ring_step(1)
    theirs = lax.ppermute(sent, axis, swap)
    before, kv_next, theirs = lax.optimization_barrier((before, kv_next, theirs))
    ring.append(kv_next)
    last = jnp.where(core == 1, ring[half], ring[half - 1])
    running = take(running, range(0, width, 2), mine)
    running = take(running, range(1, width - 2, 2), theirs)
    after = (before.astype(jnp.float32) * gain[:, None, None] + state).astype(jnp.bfloat16)
    split = after.size // HEAD_DIM
    both = jnp.concatenate([after.reshape(-1, HEAD_DIM), last.reshape(-1, HEAD_DIM)])
    both = lax.ppermute(both, axis, swap)
    both, running = lax.optimization_barrier((both, running))
    after = both[:split].reshape(after.shape)
    last = both[split:].reshape(last.shape)
    running = take(running, [width - 1], last[None])
    return jnp.where(core == 0, before, after), running


def butterfly_sum(x, axis):
    count = lax.axis_size(axis)
    step = 1
    while step < count:
        x = x + lax.ppermute(x, axis, [(i, i ^ step) for i in range(count)])
        step *= 2
    return x


def lightning_local(light_q, light_k, light_v, log_decay, joined):
    tok_rows, feat_width = light_q.shape
    head_count = feat_width // HEAD_DIM
    queries = light_q.reshape(tok_rows, head_count, HEAD_DIM)
    key_rows = light_k.reshape(tok_rows, head_count, HEAD_DIM)
    value_rows = light_v.reshape(tok_rows, head_count, HEAD_DIM)
    levels = jnp.cumsum(log_decay, axis=1)
    offsets = jnp.arange(tok_rows, dtype=jnp.int32)
    allowed = offsets[:, None] >= offsets[None, :]
    decays = jnp.exp(jnp.where(allowed[None], levels[:, :, None] - levels[:, None, :], NEG_FLOOR))
    scores = jnp.einsum("thd,shd->hts", queries, key_rows, preferred_element_type=jnp.float32)
    weights = (scores * decays).astype(jnp.bfloat16)
    intra_part = jnp.einsum("hts,shd->thd", weights, value_rows, preferred_element_type=jnp.float32)
    tail_gain = jnp.exp(levels[:, tok_rows - 1 : tok_rows] - levels)
    keyed = (key_rows * tail_gain.T[:, :, None]).astype(jnp.bfloat16)
    local_state = jnp.einsum("shd,she->hde", keyed, value_rows, preferred_element_type=jnp.float32)
    carry_gain = jnp.where(joined, jnp.exp(levels[:, tok_rows - 1]), 0.0)
    reach_gain = jnp.where(joined, jnp.exp(levels), 0.0)
    return (intra_part, (carry_gain, local_state), reach_gain, queries)


def absorb(running, queries, key_rows, value_rows, allowed):
    row_max, row_mass, weighted = running
    scores = jnp.einsum(
        "tkgd,skd->tkgs", queries, key_rows, preferred_element_type=jnp.float32
    ) * HEAD_DIM ** (-0.5)
    scores = jnp.where(allowed[:, None, None, :], scores, MASK_FILL)
    new_max = jnp.maximum(row_max, jnp.max(scores, axis=-1))
    exponent = jnp.exp(scores - new_max[..., None])
    shrink = jnp.exp(row_max - new_max)
    row_mass = row_mass * shrink + jnp.sum(exponent, axis=-1)
    update = jnp.einsum(
        "tkgs,skd->tkgd",
        exponent.astype(jnp.bfloat16),
        value_rows,
        preferred_element_type=jnp.float32,
    )
    weighted = weighted * shrink[..., None] + update
    return (new_max, row_mass, weighted)


def body(light_q, light_k, light_v, log_decay, light_gain, soft_q, soft_k, soft_v, segment_ids):
    tok_rows = light_q.shape[0]
    assert tok_rows == BLOCK
    position = lax.axis_index(("grp", "seq"))
    here_seg = segment_ids[position]
    joined = (position > 0) & (segment_ids[jnp.maximum(position - 1, 0)] == here_seg)
    intra_part, element, reach_gain, queries = lightning_local(
        light_q, light_k, light_v, log_decay, joined
    )
    core = position % 2
    window_len = WINDOW_DEV
    kv_heads = soft_k.shape[1] // HEAD_DIM
    group_size = soft_q.shape[1] // soft_k.shape[1]
    soft_queries = soft_q.reshape(tok_rows, kv_heads, group_size, HEAD_DIM)

    causal = jnp.arange(tok_rows)[:, None] >= jnp.arange(tok_rows)[None, :]

    def take(running, slot_list, chosen):
        key_rows = chosen[:, 0].reshape(-1, kv_heads, HEAD_DIM)
        value_rows = chosen[:, 1].reshape(-1, kv_heads, HEAD_DIM)
        allowed = jnp.concatenate(
            [
                causal
                if source == 0
                else jnp.broadcast_to(
                    (position >= source)
                    & (segment_ids[jnp.maximum(position - source, 0)] == here_seg),
                    causal.shape,
                )
                for source in slot_list
            ],
            axis=1,
        )
        return absorb(running, soft_queries, key_rows, value_rows, allowed)

    running = (
        jnp.full((tok_rows, kv_heads, group_size), MASK_FILL, jnp.float32),
        jnp.zeros((tok_rows, kv_heads, group_size), jnp.float32),
        jnp.zeros((tok_rows, kv_heads, group_size, HEAD_DIM), jnp.float32),
    )
    state_rounded, running = exchange(
        element, jnp.stack([soft_k, soft_v]), ("grp", "seq"), core, window_len, take, running
    )
    inter_part = (
        jnp.einsum("thd,hde->the", queries, state_rounded, preferred_element_type=jnp.float32)
        * reach_gain.T[:, :, None]
    )
    mixed = (intra_part + inter_part).reshape(tok_rows, -1)
    square_sum = butterfly_sum(jnp.sum(mixed * mixed, axis=1), "head")
    inv_norm = lax.rsqrt(square_sum / (LIGHTNING_HEADS * HEAD_DIM) + 1e-06)
    light_out = (mixed * inv_norm[:, None] * light_gain).astype(jnp.bfloat16)
    _, row_mass, weighted = running
    soft_out = (weighted / row_mass[..., None]).reshape(tok_rows, -1).astype(jnp.bfloat16)
    return (light_out, soft_out)


def solution(mesh):
    placed = (
        P(("grp", "seq"), "head"),
        P(("grp", "seq"), "head"),
        P(("grp", "seq"), "head"),
        P("head", ("grp", "seq")),
        P("head"),
        P(("grp", "seq"), "head"),
        P(("grp", "seq"), "head"),
        P(("grp", "seq"), "head"),
        P(),
    )

    return jax.shard_map(
        body,
        mesh=mesh,
        in_specs=placed,
        out_specs=(P(("grp", "seq"), "head"), P(("grp", "seq"), "head")),
        check_vma=False,
    )
```

```python
import jax
import jax.numpy as jnp
from jax import lax
from jax.sharding import PartitionSpec as P


LIGHTNING_HEADS = 32
HEAD_DIM = 128
BLOCK = 128
WINDOW_DEV = 8


NEG_FLOOR = -10000.0
MASK_FILL = -1e30


def shift_pairs(count, by, parity=None):
    return [
        (i, i + by)
        for i in range(count)
        if 0 <= i + by < count and (parity is None or i % 2 == parity)
    ]


def exchange(element, kv_pair, axis, core, width, take, running):
    count = lax.axis_size(axis)
    half = width // 2
    swap = [(i, i ^ 1) for i in range(count)]
    ring = [kv_pair]

    def ring_step(parity=None):
        return lax.ppermute(ring[-1], axis, shift_pairs(count, 2, parity))

    gain, state = element
    rows = state.shape[1]
    packed = jnp.concatenate([state, jnp.broadcast_to(gain[:, None, None], state[:, :1].shape)], 1)
    kv_next = ring_step()
    got = lax.ppermute(packed, axis, shift_pairs(count, 1, 0))
    got, kv_next = lax.optimization_barrier((got, kv_next))
    ring.append(kv_next)
    wide_state = got[:, :rows] * gain[:, None, None] + state
    wide_gain = got[:, rows, 0] * gain
    high = wide_gain.astype(jnp.bfloat16)
    low = (wide_gain - high.astype(jnp.float32)).astype(jnp.bfloat16)
    packed = jnp.concatenate(
        [
            wide_state.astype(jnp.bfloat16),
            jnp.broadcast_to(high[:, None, None], state[:, :1].shape),
            jnp.broadcast_to(low[:, None, None], state[:, :1].shape),
        ],
        1,
    )
    got = lax.ppermute(packed, axis, shift_pairs(count, 2, 1))
    got, kv_next = lax.optimization_barrier((got, ring_step()))
    ring.append(kv_next)
    got_gain = got[:, rows, 0].astype(jnp.float32) + got[:, rows + 1, 0].astype(jnp.float32)
    wide_state = got[:, :rows].astype(jnp.float32) * wide_gain[:, None, None] + wide_state
    wide_gain = got_gain * wide_gain
    got = lax.ppermute(wide_state.astype(jnp.bfloat16), axis, shift_pairs(count, 4, 1))
    kv_next = ring_step()
    got, kv_next = lax.optimization_barrier((got, kv_next))
    ring.append(kv_next)
    wide_state = got.astype(jnp.float32) * wide_gain[:, None, None] + wide_state
    mine = jnp.stack(ring[:half])
    sent = jnp.where(core == 1, jnp.stack(ring[1:half]), jnp.stack(ring[: half - 1]))
    before = lax.ppermute(wide_state.astype(jnp.bfloat16), axis, shift_pairs(count, 1, 1))
    kv_next = ring_step(1)
    theirs = lax.ppermute(sent, axis, swap)
    before, kv_next, theirs = lax.optimization_barrier((before, kv_next, theirs))
    ring.append(kv_next)
    last = jnp.where(core == 1, ring[half], ring[half - 1])
    running = take(running, range(0, width, 2), mine)
    running = take(running, range(1, width - 2, 2), theirs)
    after = (before.astype(jnp.float32) * gain[:, None, None] + state).astype(jnp.bfloat16)
    after = lax.ppermute(after, axis, shift_pairs(count, 1, 0))
    last = lax.ppermute(last, axis, swap)
    after, last, running = lax.optimization_barrier((after, last, running))
    running = take(running, [width - 1], last[None])
    return jnp.where(core == 0, before, after), running


def lightning_local(light_q, light_k, light_v, log_decay, joined):
    tok_rows, feat_width = light_q.shape
    head_count = feat_width // HEAD_DIM
    queries = light_q.reshape(tok_rows, head_count, HEAD_DIM)
    key_rows = light_k.reshape(tok_rows, head_count, HEAD_DIM)
    value_rows = light_v.reshape(tok_rows, head_count, HEAD_DIM)
    levels = jnp.cumsum(log_decay, axis=1)
    offsets = jnp.arange(tok_rows, dtype=jnp.int32)
    allowed = offsets[:, None] >= offsets[None, :]
    decays = jnp.exp(jnp.where(allowed[None], levels[:, :, None] - levels[:, None, :], NEG_FLOOR))
    scores = jnp.einsum("thd,shd->hts", queries, key_rows, preferred_element_type=jnp.float32)
    weights = (scores * decays).astype(jnp.bfloat16)
    intra_part = jnp.einsum("hts,shd->thd", weights, value_rows, preferred_element_type=jnp.float32)
    tail_gain = jnp.exp(levels[:, tok_rows - 1 : tok_rows] - levels)
    keyed = (key_rows * tail_gain.T[:, :, None]).astype(jnp.bfloat16)
    local_state = jnp.einsum("shd,she->hde", keyed, value_rows, preferred_element_type=jnp.float32)
    carry_gain = jnp.where(joined, jnp.exp(levels[:, tok_rows - 1]), 0.0)
    reach_gain = jnp.where(joined, jnp.exp(levels), 0.0)
    return (intra_part, (carry_gain, local_state), reach_gain, queries)


def absorb(running, queries, key_rows, value_rows, allowed):
    row_max, row_mass, weighted = running
    scores = jnp.einsum(
        "tkgd,skd->tkgs", queries, key_rows, preferred_element_type=jnp.float32
    ) * HEAD_DIM ** (-0.5)
    scores = jnp.where(allowed[:, None, None, :], scores, MASK_FILL)
    new_max = jnp.maximum(row_max, jnp.max(scores, axis=-1))
    exponent = jnp.exp(scores - new_max[..., None])
    shrink = jnp.exp(row_max - new_max)
    row_mass = row_mass * shrink + jnp.sum(exponent, axis=-1)
    update = jnp.einsum(
        "tkgs,skd->tkgd",
        exponent.astype(jnp.bfloat16),
        value_rows,
        preferred_element_type=jnp.float32,
    )
    weighted = weighted * shrink[..., None] + update
    return (new_max, row_mass, weighted)


def body(light_q, light_k, light_v, log_decay, light_gain, soft_q, soft_k, soft_v, segment_ids):
    tok_rows = light_q.shape[0]
    assert tok_rows == BLOCK
    position = lax.axis_index(("grp", "seq"))
    here_seg = segment_ids[position]
    joined = (position > 0) & (segment_ids[jnp.maximum(position - 1, 0)] == here_seg)
    intra_part, element, reach_gain, queries = lightning_local(
        light_q, light_k, light_v, log_decay, joined
    )
    core = position % 2
    window_len = WINDOW_DEV
    kv_heads = soft_k.shape[1] // HEAD_DIM
    group_size = soft_q.shape[1] // soft_k.shape[1]
    soft_queries = soft_q.reshape(tok_rows, kv_heads, group_size, HEAD_DIM)

    causal = jnp.arange(tok_rows)[:, None] >= jnp.arange(tok_rows)[None, :]

    def take(running, slot_list, chosen):
        key_rows = chosen[:, 0].reshape(-1, kv_heads, HEAD_DIM)
        value_rows = chosen[:, 1].reshape(-1, kv_heads, HEAD_DIM)
        allowed = jnp.concatenate(
            [
                causal
                if source == 0
                else jnp.broadcast_to(
                    (position >= source)
                    & (segment_ids[jnp.maximum(position - source, 0)] == here_seg),
                    causal.shape,
                )
                for source in slot_list
            ],
            axis=1,
        )
        return absorb(running, soft_queries, key_rows, value_rows, allowed)

    running = (
        jnp.full((tok_rows, kv_heads, group_size), MASK_FILL, jnp.float32),
        jnp.zeros((tok_rows, kv_heads, group_size), jnp.float32),
        jnp.zeros((tok_rows, kv_heads, group_size, HEAD_DIM), jnp.float32),
    )
    state_rounded, running = exchange(
        element, jnp.stack([soft_k, soft_v]), ("grp", "seq"), core, window_len, take, running
    )
    inter_part = (
        jnp.einsum("thd,hde->the", queries, state_rounded, preferred_element_type=jnp.float32)
        * reach_gain.T[:, :, None]
    )
    mixed = (intra_part + inter_part).reshape(tok_rows, -1)
    square_sum = lax.psum(jnp.sum(mixed * mixed, axis=1), "head")
    inv_norm = lax.rsqrt(square_sum / (LIGHTNING_HEADS * HEAD_DIM) + 1e-06)
    light_out = (mixed * inv_norm[:, None] * light_gain).astype(jnp.bfloat16)
    _, row_mass, weighted = running
    soft_out = (weighted / row_mass[..., None]).reshape(tok_rows, -1).astype(jnp.bfloat16)
    return (light_out, soft_out)


def solution(mesh):
    placed = (
        P(("grp", "seq"), "head"),
        P(("grp", "seq"), "head"),
        P(("grp", "seq"), "head"),
        P("head", ("grp", "seq")),
        P("head"),
        P(("grp", "seq"), "head"),
        P(("grp", "seq"), "head"),
        P(("grp", "seq"), "head"),
        P(),
    )

    return jax.shard_map(
        body,
        mesh=mesh,
        in_specs=placed,
        out_specs=(P(("grp", "seq"), "head"), P(("grp", "seq"), "head")),
        check_vma=False,
    )
```
